32 devices in a mesh: layer: 2 (over x), row: 4 (over y, core), col: 4 (over z).
Axes of the slice: x: 2, y: 2, z: 4, core: 2. Of those that a mesh axis runs over, the one named last changes fastest.
Arguments:
- left_matrix: bfloat16 [8192, 1024], P('row', ('layer', 'col')), may hold values from -6 to 6
- square_term: bfloat16 [1024, 1024], P(('layer', 'row'), 'col'), may hold values from -0.5 to 0.5
- block_pattern: int32 [64, 8], replicated, may hold values from 0 to 1, as said below
- keep_mask: int32 [64, 8], replicated, may hold values 0 or 1
Outputs:
- product: bfloat16 [8192, 1024], P('row', 'col')
The draws below stay inside these ranges and needn't reach their ends.
Inputs may be any that keep to these rules, and one draw needn't show every extreme that they name: `block_pattern`: in each aligned group of 16 block rows, every block column holds 1 to 8 stored blocks; some group holds exactly 8.
All inputs are finite; a program needn't handle non-finite values.
Results may differ from the reference program's by a relative error of at most 0.0038.
Values may be sent and summed in bfloat16 or wider, within the bound.
No kernel may reach another device: no remote copies, remote signals or barrier semaphores. Data moves between devices by JAX's collectives and lax.ppermute only.
A program may use at most 64 MiB of HBM per device.

```python
import jax
import jax.numpy as jnp
from jax import lax

BLK = 128
RB_DEV = 16
CAP = 8
M = 8192
K = 1024
N = 1024


def draw_block_pattern(key, part):
    total_rows = M // BLK
    total_cols = K // BLK
    groups = total_rows // RB_DEV
    key_count = jax.random.fold_in(key, 11)
    key_rank = jax.random.fold_in(key, 23)
    lowest = max(1, CAP // 2)
    counts = jax.random.randint(key_count, (groups, total_cols), lowest, CAP + 1)
    counts = counts.at[0, 0].set(CAP)
    scores = jax.random.randint(key_rank, (groups, total_cols, RB_DEV), 0, 2 ** 30)
    order = jnp.argsort(scores, axis=2, stable=True)
    ranks = jnp.argsort(order, axis=2, stable=True)
    chosen = (ranks < counts[:, :, None]).astype(jnp.int32)
    chosen = jnp.transpose(chosen, (0, 2, 1)).reshape(total_rows, total_cols)
    return chosen


def set_ends(entries, rng, low, top_value):
    shape = entries.shape
    place = [jax.random.randint(jax.random.fold_in(rng, axis), (), 0, shape[axis]) for axis in range(len(shape))]
    entries = entries.at[tuple(place)].set(low)
    longest = shape.index(max(shape))
    place[longest] = (place[longest] + 1) % shape[longest]
    return entries.at[tuple(place)].set(top_value)


def block_scale(own_key, extent, pieces, low, top_value):
    gain = 1.0
    for dim, parts in pieces:
        draws = jax.random.uniform(jax.random.fold_in(jax.random.fold_in(own_key, 6), dim), (parts,), jnp.float32, low / len(pieces), top_value / len(pieces))
        gain = gain * jnp.repeat(jnp.exp(draws), extent[dim] // parts).reshape((-1,) + (1,) * (len(extent) - 1 - dim))
    return gain


def centred(key, extent, width, limit, cuts=(), dtype=jnp.bfloat16):
    gain = block_scale(key, extent, cuts, -0.22, 0.18) if cuts else 1.0
    drawn = jax.random.normal(key, extent, jnp.float32) * width * gain
    return jnp.minimum(jnp.maximum(drawn, -limit), limit).astype(dtype)


def setup_inputs(seed: int = 0) -> dict:
    key_of = jax.random.split(jax.random.key(seed), 5)
    return {
        "left_matrix": centred(key_of[0], (M, K), 1.0, 6.0, ((0, 4), (1, 8))),
        "square_term": centred(key_of[1], (K, N), (K // 8) ** -0.5, 0.5, ((0, 8), (1, 4))),
        "block_pattern": draw_block_pattern(jax.random.fold_in(key_of[4], 71), 0),
        "keep_mask": set_ends((jax.random.randint(key_of[3], (M // BLK, N // BLK), 0, 4) < 3).astype(jnp.int32), jax.random.fold_in(key_of[3], 1), 0, 1),
    }


def expand(mask_blocks):
    return jnp.repeat(jnp.repeat(mask_blocks, BLK, axis=0), BLK, axis=1)


def reference(left_matrix, square_term, block_pattern, keep_mask):
    sparse_left = jnp.where(expand(block_pattern) > 0, left_matrix, jnp.zeros_like(left_matrix))
    row_index = lax.broadcasted_iota(jnp.int32, (K, N), 0)
    col_index = lax.broadcasted_iota(jnp.int32, (K, N), 1)
    unit = jnp.where(row_index == col_index, jnp.float32(1.5), jnp.float32(0.0))
    right_factor = (unit - 0.5 * square_term.astype(jnp.float32)).astype(jnp.bfloat16)
    full_sum = jnp.dot(sparse_left.astype(jnp.float32), right_factor.astype(jnp.float32), precision=lax.Precision.HIGHEST, preferred_element_type=jnp.float32)
    kept = jnp.where(expand(keep_mask) > 0, full_sum, jnp.zeros_like(full_sum))
    return kept.astype(jnp.bfloat16)
```

```python
import jax
import jax.numpy as jnp
from jax import lax
from jax.sharding import PartitionSpec as P

BLK = 128
GROUP = 16
CAP = 8


def slot_table(pattern):
    stored = (pattern > 0).astype(jnp.int32)
    rows = pattern.shape[0]
    groups = rows // GROUP
    grouped = stored.reshape(groups, GROUP, -1)
    slot = jnp.cumsum(grouped, axis=1) - 1
    group_base = (jnp.arange(groups, dtype=jnp.int32) * CAP)[:, None, None]
    slot = (slot + group_base).reshape(rows, -1)
    return stored, slot


def per_device(left_matrix, square_term, block_pattern, keep_mask):
    row_idx = lax.axis_index("row")
    col_idx = lax.axis_index("col")
    layer_idx = lax.axis_index("layer")
    row_count = lax.axis_size("row")
    col_count = lax.axis_size("col")
    rows_local = left_matrix.shape[0]
    row_blocks = rows_local // BLK
    inner_blocks = left_matrix.shape[1] // BLK
    inner_local = square_term.shape[0]
    cols_local = square_term.shape[1]
    col_blocks = cols_local // BLK
    slots = (row_blocks // GROUP) * CAP
    total_inner_blocks = block_pattern.shape[1]

    inner_start = (layer_idx * col_count + col_idx) * inner_blocks
    pattern_patch = lax.dynamic_slice(
        block_pattern, (row_idx * row_blocks, inner_start), (row_blocks, inner_blocks)
    )
    stored, slot = slot_table(pattern_patch)
    slot_ids = jnp.arange(slots, dtype=jnp.int32)
    hit = (stored[:, :, None] > 0) & (slot[:, :, None] == slot_ids[None, None, :])
    source_row = jnp.sum(
        jnp.where(hit, jnp.arange(row_blocks, dtype=jnp.int32)[:, None, None], 0), axis=0
    )
    blocks = left_matrix.reshape(row_blocks, BLK, inner_blocks, BLK).transpose(2, 0, 1, 3)
    flat_blocks = blocks.reshape(inner_blocks * row_blocks, BLK, BLK)
    take_idx = source_row + (jnp.arange(inner_blocks, dtype=jnp.int32) * row_blocks)[:, None]
    packed = jnp.take(flat_blocks, take_idx.reshape(-1), axis=0)
    packed = packed.reshape(inner_blocks, slots, BLK, BLK)

    gathered = lax.all_gather(packed, ("layer", "col"), axis=0, tiled=True)

    first_inner = (layer_idx * row_count + row_idx) * inner_local
    first_col = col_idx * cols_local
    inner_pos = first_inner + lax.broadcasted_iota(jnp.int32, (inner_local, cols_local), 0)
    col_pos = first_col + lax.broadcasted_iota(jnp.int32, (inner_local, cols_local), 1)
    unit = jnp.where(inner_pos == col_pos, jnp.float32(1.5), jnp.float32(0.0))
    right_factor = (unit - 0.5 * square_term.astype(jnp.float32)).astype(jnp.bfloat16)
    right_full = lax.all_gather(right_factor, ("layer", "row"), axis=0, tiled=True)

    panel_pattern = lax.dynamic_slice(
        block_pattern, (row_idx * row_blocks, 0), (row_blocks, total_inner_blocks)
    )
    p_stored, p_slot = slot_table(panel_pattern)
    gather_idx = (
        jnp.arange(total_inner_blocks, dtype=jnp.int32)[None, :] * slots
        + jnp.clip(p_slot, 0, slots - 1)
    )
    flat_packed = gathered.reshape(total_inner_blocks * slots, BLK, BLK)
    right_blocks = right_full.reshape(total_inner_blocks, BLK, cols_local)

    def chunk_sum(first, count):
        idx = lax.dynamic_slice_in_dim(gather_idx, first, count, axis=1)
        keep = lax.dynamic_slice_in_dim(p_stored, first, count, axis=1)
        dense = jnp.take(flat_packed, idx.reshape(-1), axis=0)
        dense = dense.reshape(row_blocks, count, BLK, BLK)
        dense = jnp.where(keep[:, :, None, None] > 0, dense, jnp.zeros_like(dense))
        rhs = lax.dynamic_slice_in_dim(right_blocks, first, count, axis=0)
        return jnp.einsum("ijab,jbc->iac", dense, rhs, preferred_element_type=jnp.float32)

    dense_bytes = row_blocks * total_inner_blocks * BLK * BLK * 2
    chunks = max(1, dense_bytes // (4 << 20))
    while total_inner_blocks % chunks:
        chunks += 1
    if chunks == 1:
        full_sum = chunk_sum(0, total_inner_blocks)
    else:
        per_chunk = total_inner_blocks // chunks

        def body(c, acc):
            return acc + chunk_sum(c * per_chunk, per_chunk)

        full_sum = lax.fori_loop(
            0, chunks, body, jnp.zeros((row_blocks, BLK, cols_local), jnp.float32)
        )
    full_sum = full_sum.reshape(rows_local, cols_local)

    keep_patch = lax.dynamic_slice(
        keep_mask, (row_idx * row_blocks, col_idx * col_blocks), (row_blocks, col_blocks)
    )
    keep_full = jnp.repeat(jnp.repeat(keep_patch, BLK, axis=0), BLK, axis=1)
    kept = jnp.where(keep_full > 0, full_sum, jnp.zeros_like(full_sum))
    return kept.astype(jnp.bfloat16)


def solution(mesh):
    return jax.shard_map(
        per_device,
        mesh=mesh,
        in_specs=(P("row", ("layer", "col")), P(("layer", "row"), "col"), P(), P()),
        out_specs=P("row", "col"),
        check_vma=False,
    )
```

```python
import jax
import jax.numpy as jnp
from jax import lax
from jax.sharding import PartitionSpec as P

BLK = 128
GROUP = 16
CAP = 8


def slot_table(pattern):
    stored = (pattern > 0).astype(jnp.int32)
    rows = pattern.shape[0]
    groups = rows // GROUP
    grouped = stored.reshape(groups, GROUP, -1)
    slot = jnp.cumsum(grouped, axis=1) - 1
    group_base = (jnp.arange(groups, dtype=jnp.int32) * CAP)[:, None, None]
    slot = (slot + group_base).reshape(rows, -1)
    return stored, slot


def ring_gather(x, axis, index, count):
    pieces = [x]
    for k in range(1, count):
        perm = [(s, (s + k) % count) for s in range(count)]
        pieces.append(lax.ppermute(x, axis, perm))
    sources = [(index - k) % count for k in range(count)]
    return pieces, sources


def ring_gather_list(xs, axis, index, count):
    out, sources = [], []
    for x in xs:
        got, src = ring_gather(x, axis, index, count)
        out.extend(got)
        sources.extend(src)
    return out, sources


def per_device(left_matrix, square_term, block_pattern, keep_mask):
    row_idx = lax.axis_index("row")
    col_idx = lax.axis_index("col")
    layer_idx = lax.axis_index("layer")
    row_count = lax.axis_size("row")
    col_count = lax.axis_size("col")
    rows_local = left_matrix.shape[0]
    row_blocks = rows_local // BLK
    inner_blocks = left_matrix.shape[1] // BLK
    inner_local = square_term.shape[0]
    cols_local = square_term.shape[1]
    col_blocks = cols_local // BLK
    slots = (row_blocks // GROUP) * CAP
    total_inner_blocks = block_pattern.shape[1]

    inner_start = (layer_idx * col_count + col_idx) * inner_blocks
    pattern_patch = lax.dynamic_slice(
        block_pattern, (row_idx * row_blocks, inner_start), (row_blocks, inner_blocks)
    )
    stored, slot = slot_table(pattern_patch)
    slot_ids = jnp.arange(slots, dtype=jnp.int32)
    hit = (stored[:, :, None] > 0) & (slot[:, :, None] == slot_ids[None, None, :])
    source_row = jnp.sum(
        jnp.where(hit, jnp.arange(row_blocks, dtype=jnp.int32)[:, None, None], 0), axis=0
    )
    blocks = left_matrix.reshape(row_blocks, BLK, inner_blocks, BLK).transpose(2, 0, 1, 3)
    flat_blocks = blocks.reshape(inner_blocks * row_blocks, BLK, BLK)
    take_idx = source_row + (jnp.arange(inner_blocks, dtype=jnp.int32) * row_blocks)[:, None]
    packed = jnp.take(flat_blocks, take_idx.reshape(-1), axis=0)
    packed = packed.reshape(inner_blocks, slots, BLK, BLK)

    layer_count = lax.axis_size("layer")
    use_permutes = inner_blocks == 1 and col_count <= 4 and row_count <= 4 and layer_count <= 2
    if use_permutes:
        pieces, piece_col = ring_gather(packed, "col", col_idx, col_count)
        pieces, piece_layer = ring_gather_list(pieces, "layer", layer_idx, layer_count)
        piece_col = [piece_col[k] for k in range(col_count) for m in range(layer_count)]
        piece_j = jnp.stack(
            [pl_ * col_count + pc for pl_, pc in zip(piece_layer, piece_col)]
        ).astype(jnp.int32)
        gathered = jnp.concatenate(pieces, axis=0)
    else:
        gathered = lax.all_gather(packed, ("layer", "col"), axis=0, tiled=True)
        piece_j = jnp.arange(total_inner_blocks, dtype=jnp.int32)

    first_inner = (layer_idx * row_count + row_idx) * inner_local
    first_col = col_idx * cols_local
    inner_pos = first_inner + lax.broadcasted_iota(jnp.int32, (inner_local, cols_local), 0)
    col_pos = first_col + lax.broadcasted_iota(jnp.int32, (inner_local, cols_local), 1)
    unit = jnp.where(inner_pos == col_pos, jnp.float32(1.5), jnp.float32(0.0))
    right_factor = (unit - 0.5 * square_term.astype(jnp.float32)).astype(jnp.bfloat16)
    if use_permutes:
        rf_pieces, rf_row = ring_gather(right_factor[None], "row", row_idx, row_count)
        rf_pieces, rf_layer = ring_gather_list(rf_pieces, "layer", layer_idx, layer_count)
        rf_stack = jnp.concatenate(rf_pieces, axis=0)
        q = jnp.arange(layer_count * row_count, dtype=jnp.int32)
        shift_r = (row_idx - q % row_count) % row_count
        shift_l = (layer_idx - q // row_count) % layer_count
        right_full = jnp.take(rf_stack, shift_r * layer_count + shift_l, axis=0)
        right_full = right_full.reshape(layer_count * row_count * inner_local, cols_local)
    else:
        right_full = lax.all_gather(right_factor, ("layer", "row"), axis=0, tiled=True)

    panel_pattern = lax.dynamic_slice(
        block_pattern, (row_idx * row_blocks, 0), (row_blocks, total_inner_blocks)
    )
    p_stored, p_slot = slot_table(panel_pattern)
    p_stored = jnp.take(p_stored, piece_j, axis=1)
    p_slot = jnp.take(p_slot, piece_j, axis=1)
    gather_idx = (
        jnp.arange(total_inner_blocks, dtype=jnp.int32)[None, :] * slots
        + jnp.clip(p_slot, 0, slots - 1)
    )
    flat_packed = gathered.reshape(total_inner_blocks * slots, BLK, BLK)
    right_blocks = jnp.take(right_full.reshape(total_inner_blocks, BLK, cols_local), piece_j, axis=0)

    def chunk_sum(first, count):
        idx = lax.dynamic_slice_in_dim(gather_idx, first, count, axis=1)
        keep = lax.dynamic_slice_in_dim(p_stored, first, count, axis=1)
        dense = jnp.take(flat_packed, idx.reshape(-1), axis=0)
        dense = dense.reshape(row_blocks, count, BLK, BLK)
        dense = jnp.where(keep[:, :, None, None] > 0, dense, jnp.zeros_like(dense))
        rhs = lax.dynamic_slice_in_dim(right_blocks, first, count, axis=0)
        return jnp.einsum("ijab,jbc->iac", dense, rhs, preferred_element_type=jnp.float32)

    dense_bytes = row_blocks * total_inner_blocks * BLK * BLK * 2
    chunks = max(1, dense_bytes // (4 << 20))
    while total_inner_blocks % chunks:
        chunks += 1
    if chunks == 1:
        full_sum = chunk_sum(0, total_inner_blocks)
    else:
        per_chunk = total_inner_blocks // chunks

        def body(c, acc):
            return acc + chunk_sum(c * per_chunk, per_chunk)

        full_sum = lax.fori_loop(
            0, chunks, body, jnp.zeros((row_blocks, BLK, cols_local), jnp.float32)
        )
    full_sum = full_sum.reshape(rows_local, cols_local)

    keep_patch = lax.dynamic_slice(
        keep_mask, (row_idx * row_blocks, col_idx * col_blocks), (row_blocks, col_blocks)
    )
    keep_full = jnp.repeat(jnp.repeat(keep_patch, BLK, axis=0), BLK, axis=1)
    kept = jnp.where(keep_full > 0, full_sum, jnp.zeros_like(full_sum))
    return kept.astype(jnp.bfloat16)


def solution(mesh):
    return jax.shard_map(
        per_device,
        mesh=mesh,
        in_specs=(P("row", ("layer", "col")), P(("layer", "row"), "col"), P(), P()),
        out_specs=P("row", "col"),
        check_vma=False,
    )
```

```python
import functools

import jax
import jax.numpy as jnp
from jax import lax
from jax.experimental import pallas as pl
from jax.experimental.pallas import tpu as pltpu
from jax.sharding import PartitionSpec as P

BLK = 128
GROUP = 16
CAP = 8


def slot_table(pattern):
    stored = (pattern > 0).astype(jnp.int32)
    rows = pattern.shape[0]
    groups = rows // GROUP
    grouped = stored.reshape(groups, GROUP, -1)
    slot = jnp.cumsum(grouped, axis=1) - 1
    group_base = (jnp.arange(groups, dtype=jnp.int32) * CAP)[:, None, None]
    slot = (slot + group_base).reshape(rows, -1)
    return stored, slot


def ring_gather(x, axis, index, count):
    pieces = [x]
    for k in range(1, count):
        perm = [(s, (s + k) % count) for s in range(count)]
        pieces.append(lax.ppermute(x, axis, perm))
    sources = [(index - k) % count for k in range(count)]
    return pieces, sources


def ring_gather_list(xs, axis, index, count):
    out, sources = [], []
    for x in xs:
        got, src = ring_gather(x, axis, index, count)
        out.extend(got)
        sources.extend(src)
    return out, sources


def product_kernel(slot_ref, rf_pos_ref, keep_ref, *refs, pieces, row_blocks, cols):
    left_refs = refs[:pieces]
    rf_refs = refs[pieces:2 * pieces]
    out_ref = refs[2 * pieces]
    lhs_scr, rf_scr = refs[2 * pieces + 1:]
    for q in range(pieces):
        at = pl.multiple_of(rf_pos_ref[q] * BLK, BLK)
        rf_scr[pl.ds(at, BLK), :] = rf_refs[q][...]
    for p in range(pieces):
        for i in range(row_blocks):
            s = slot_ref[p, i]
            blk = left_refs[p][jnp.maximum(s, 0)]
            blk = jnp.where(s >= 0, blk, jnp.zeros_like(blk))
            lhs_scr[i * BLK:(i + 1) * BLK, p * BLK:(p + 1) * BLK] = blk
    tile = 2 * BLK
    for t in range(row_blocks * BLK // tile):
        res = jnp.dot(
            lhs_scr[t * tile:(t + 1) * tile, :], rf_scr[...], preferred_element_type=jnp.float32
        )
        for a in range(tile // BLK):
            i = t * (tile // BLK) + a
            for b in range(cols // BLK):
                sub = res[a * BLK:(a + 1) * BLK, b * BLK:(b + 1) * BLK]
                sub = jnp.where(keep_ref[i, b] > 0, sub, jnp.zeros_like(sub))
                out_ref[i * BLK:(i + 1) * BLK, b * BLK:(b + 1) * BLK] = sub.astype(out_ref.dtype)


def product_call(slot_tbl, rf_pos, keep_patch, left_pieces, rf_pieces):
    pieces = len(left_pieces)
    row_blocks = slot_tbl.shape[1]
    cols = rf_pieces[0].shape[1]
    smem = pl.BlockSpec(memory_space=pltpu.SMEM)
    vmem = pl.BlockSpec(memory_space=pltpu.VMEM)
    flops = 2 * row_blocks * BLK * pieces * BLK * cols
    bytes_accessed = pieces * (left_pieces[0].size + rf_pieces[0].size) * 2 + row_blocks * BLK * cols * 2
    return pl.pallas_call(
        functools.partial(product_kernel, pieces=pieces, row_blocks=row_blocks, cols=cols),
        out_shape=jax.ShapeDtypeStruct((row_blocks * BLK, cols), jnp.bfloat16),
        in_specs=[smem, smem, smem] + [vmem] * (2 * pieces),
        out_specs=vmem,
        scratch_shapes=[
            pltpu.VMEM((row_blocks * BLK, pieces * BLK), jnp.bfloat16),
            pltpu.VMEM((pieces * BLK, cols), jnp.bfloat16),
        ],
        cost_estimate=pl.CostEstimate(flops=flops, bytes_accessed=bytes_accessed, transcendentals=0),
    )(slot_tbl, rf_pos, keep_patch, *left_pieces, *rf_pieces)


def per_device(left_matrix, square_term, block_pattern, keep_mask):
    row_idx = lax.axis_index("row")
    col_idx = lax.axis_index("col")
    layer_idx = lax.axis_index("layer")
    row_count = lax.axis_size("row")
    col_count = lax.axis_size("col")
    rows_local = left_matrix.shape[0]
    row_blocks = rows_local // BLK
    inner_blocks = left_matrix.shape[1] // BLK
    inner_local = square_term.shape[0]
    cols_local = square_term.shape[1]
    col_blocks = cols_local // BLK
    slots = (row_blocks // GROUP) * CAP
    total_inner_blocks = block_pattern.shape[1]

    inner_start = (layer_idx * col_count + col_idx) * inner_blocks
    pattern_patch = lax.dynamic_slice(
        block_pattern, (row_idx * row_blocks, inner_start), (row_blocks, inner_blocks)
    )
    stored, slot = slot_table(pattern_patch)
    slot_ids = jnp.arange(slots, dtype=jnp.int32)
    hit = (stored[:, :, None] > 0) & (slot[:, :, None] == slot_ids[None, None, :])
    source_row = jnp.sum(
        jnp.where(hit, jnp.arange(row_blocks, dtype=jnp.int32)[:, None, None], 0), axis=0
    )
    blocks = left_matrix.reshape(row_blocks, BLK, inner_blocks, BLK).transpose(2, 0, 1, 3)
    flat_blocks = blocks.reshape(inner_blocks * row_blocks, BLK, BLK)
    take_idx = source_row + (jnp.arange(inner_blocks, dtype=jnp.int32) * row_blocks)[:, None]
    packed = jnp.take(flat_blocks, take_idx.reshape(-1), axis=0)
    packed = packed.reshape(inner_blocks, slots, BLK, BLK)

    layer_count = lax.axis_size("layer")
    keep_patch = lax.dynamic_slice(
        keep_mask, (row_idx * row_blocks, col_idx * col_blocks), (row_blocks, col_blocks)
    ).astype(jnp.int32)
    panel_pattern = lax.dynamic_slice(
        block_pattern, (row_idx * row_blocks, 0), (row_blocks, total_inner_blocks)
    )

    first_inner = (layer_idx * row_count + row_idx) * inner_local
    first_col = col_idx * cols_local
    inner_pos = first_inner + lax.broadcasted_iota(jnp.int32, (inner_local, cols_local), 0)
    col_pos = first_col + lax.broadcasted_iota(jnp.int32, (inner_local, cols_local), 1)
    unit = jnp.where(inner_pos == col_pos, jnp.float32(1.5), jnp.float32(0.0))
    right_factor = (unit - 0.5 * square_term.astype(jnp.float32)).astype(jnp.bfloat16)

    use_permutes = (
        inner_blocks == 1
        and inner_local == BLK
        and col_count == row_count
        and col_count <= 4
        and layer_count <= 2
    )
    if use_permutes:
        pieces, piece_col = ring_gather(packed[0], "col", col_idx, col_count)
        pieces, piece_layer = ring_gather_list(pieces, "layer", layer_idx, layer_count)
        piece_col = [piece_col[k] for k in range(col_count) for m in range(layer_count)]
        piece_j = jnp.stack(
            [src_l * col_count + src_c for src_l, src_c in zip(piece_layer, piece_col)]
        ).astype(jnp.int32)
        rf_pieces, rf_row = ring_gather(right_factor, "row", row_idx, row_count)
        rf_pieces, rf_layer = ring_gather_list(rf_pieces, "layer", layer_idx, layer_count)
        rf_row = [rf_row[k] for k in range(row_count) for m in range(layer_count)]
        rf_q = jnp.stack(
            [src_l * row_count + src_r for src_l, src_r in zip(rf_layer, rf_row)]
        ).astype(jnp.int32)
        rf_pos = ((col_idx - rf_q % col_count) % col_count) * layer_count + (
            (layer_idx - rf_q // col_count) % layer_count
        )
        p_stored, p_slot = slot_table(panel_pattern)
        slot_tbl = jnp.where(p_stored > 0, p_slot, -1)
        slot_tbl = jnp.take(slot_tbl, piece_j, axis=1).T.astype(jnp.int32)
        return product_call(slot_tbl, rf_pos.astype(jnp.int32), keep_patch, pieces, rf_pieces)

    gathered = lax.all_gather(packed, ("layer", "col"), axis=0, tiled=True)
    piece_j = jnp.arange(total_inner_blocks, dtype=jnp.int32)
    right_full = lax.all_gather(right_factor, ("layer", "row"), axis=0, tiled=True)

    p_stored, p_slot = slot_table(panel_pattern)
    p_stored = jnp.take(p_stored, piece_j, axis=1)
    p_slot = jnp.take(p_slot, piece_j, axis=1)
    gather_idx = (
        jnp.arange(total_inner_blocks, dtype=jnp.int32)[None, :] * slots
        + jnp.clip(p_slot, 0, slots - 1)
    )
    flat_packed = gathered.reshape(total_inner_blocks * slots, BLK, BLK)
    right_blocks = jnp.take(right_full.reshape(total_inner_blocks, BLK, cols_local), piece_j, axis=0)

    def chunk_sum(first, count):
        idx = lax.dynamic_slice_in_dim(gather_idx, first, count, axis=1)
        keep = lax.dynamic_slice_in_dim(p_stored, first, count, axis=1)
        dense = jnp.take(flat_packed, idx.reshape(-1), axis=0)
        dense = dense.reshape(row_blocks, count, BLK, BLK)
        dense = jnp.where(keep[:, :, None, None] > 0, dense, jnp.zeros_like(dense))
        rhs = lax.dynamic_slice_in_dim(right_blocks, first, count, axis=0)
        return jnp.einsum("ijab,jbc->iac", dense, rhs, preferred_element_type=jnp.float32)

    dense_bytes = row_blocks * total_inner_blocks * BLK * BLK * 2
    chunks = max(1, dense_bytes // (4 << 20))
    while total_inner_blocks % chunks:
        chunks += 1
    if chunks == 1:
        full_sum = chunk_sum(0, total_inner_blocks)
    else:
        per_chunk = total_inner_blocks // chunks

        def body(c, acc):
            return acc + chunk_sum(c * per_chunk, per_chunk)

        full_sum = lax.fori_loop(
            0, chunks, body, jnp.zeros((row_blocks, BLK, cols_local), jnp.float32)
        )
    full_sum = full_sum.reshape(rows_local, cols_local)

    keep_full = jnp.repeat(jnp.repeat(keep_patch, BLK, axis=0), BLK, axis=1)
    kept = jnp.where(keep_full > 0, full_sum, jnp.zeros_like(full_sum))
    return kept.astype(jnp.bfloat16)


def solution(mesh):
    return jax.shard_map(
        per_device,
        mesh=mesh,
        in_specs=(P("row", ("layer", "col")), P(("layer", "row"), "col"), P(), P()),
        out_specs=P("row", "col"),
        check_vma=False,
    )
```

```python
import functools

import jax
import jax.numpy as jnp
from jax import lax
from jax.experimental import pallas as pl
from jax.experimental.pallas import tpu as pltpu
from jax.sharding import PartitionSpec as P

BLK = 128
GROUP = 16
CAP = 8


def slot_table(pattern):
    stored = (pattern > 0).astype(jnp.int32)
    rows = pattern.shape[0]
    groups = rows // GROUP
    grouped = stored.reshape(groups, GROUP, -1)
    slot = jnp.cumsum(grouped, axis=1) - 1
    group_base = (jnp.arange(groups, dtype=jnp.int32) * CAP)[:, None, None]
    slot = (slot + group_base).reshape(rows, -1)
    return stored, slot


def ring_gather(x, axis, index, count):
    pieces = [x]
    for k in range(1, count):
        perm = [(s, (s + k) % count) for s in range(count)]
        pieces.append(lax.ppermute(x, axis, perm))
    sources = [(index - k) % count for k in range(count)]
    return pieces, sources


def ring_gather_list(xs, axis, index, count):
    out, sources = [], []
    for x in xs:
        got, src = ring_gather(x, axis, index, count)
        out.extend(got)
        sources.extend(src)
    return out, sources


def product_kernel(slot_ref, rf_pos_ref, keep_ref, *refs, pieces, rf_groups, row_blocks, cols):
    left_refs = refs[:pieces]
    rf_refs = refs[pieces:pieces + rf_groups]
    out_ref = refs[pieces + rf_groups]
    lhs_scr, rf_scr = refs[pieces + rf_groups + 1:]
    per_group = pieces // rf_groups
    for q in range(pieces):
        at = pl.multiple_of(rf_pos_ref[q] * BLK, BLK)
        rf_scr[pl.ds(at, BLK), :] = rf_refs[q // per_group][q % per_group]
    for p in range(pieces):
        for i in range(row_blocks):
            s = slot_ref[p, i]
            blk = left_refs[p][jnp.maximum(s, 0)]
            blk = jnp.where(s >= 0, blk, jnp.zeros_like(blk))
            lhs_scr[i * BLK:(i + 1) * BLK, p * BLK:(p + 1) * BLK] = blk
    tile = 2 * BLK
    for t in range(row_blocks * BLK // tile):
        res = jnp.dot(
            lhs_scr[t * tile:(t + 1) * tile, :], rf_scr[...], preferred_element_type=jnp.float32
        )
        for a in range(tile // BLK):
            i = t * (tile // BLK) + a
            for b in range(cols // BLK):
                sub = res[a * BLK:(a + 1) * BLK, b * BLK:(b + 1) * BLK]
                sub = jnp.where(keep_ref[i, b] > 0, sub, jnp.zeros_like(sub))
                out_ref[i * BLK:(i + 1) * BLK, b * BLK:(b + 1) * BLK] = sub.astype(out_ref.dtype)


def product_call(slot_tbl, rf_pos, keep_patch, left_pieces, rf_pieces):
    pieces = len(left_pieces)
    rf_groups = len(rf_pieces)
    row_blocks = slot_tbl.shape[1]
    cols = rf_pieces[0].shape[-1]
    smem = pl.BlockSpec(memory_space=pltpu.SMEM)
    vmem = pl.BlockSpec(memory_space=pltpu.VMEM)
    flops = 2 * row_blocks * BLK * pieces * BLK * cols
    bytes_accessed = (
        pieces * left_pieces[0].size * 2 + rf_groups * rf_pieces[0].size * 2 + row_blocks * BLK * cols * 2
    )
    return pl.pallas_call(
        functools.partial(
            product_kernel, pieces=pieces, rf_groups=rf_groups, row_blocks=row_blocks, cols=cols
        ),
        out_shape=jax.ShapeDtypeStruct((row_blocks * BLK, cols), jnp.bfloat16),
        in_specs=[smem, smem, smem] + [vmem] * (pieces + rf_groups),
        out_specs=vmem,
        scratch_shapes=[
            pltpu.VMEM((row_blocks * BLK, pieces * BLK), jnp.bfloat16),
            pltpu.VMEM((pieces * BLK, cols), jnp.bfloat16),
        ],
        cost_estimate=pl.CostEstimate(flops=flops, bytes_accessed=bytes_accessed, transcendentals=0),
    )(slot_tbl, rf_pos, keep_patch, *left_pieces, *rf_pieces)


def per_device(left_matrix, square_term, block_pattern, keep_mask):
    row_idx = lax.axis_index("row")
    col_idx = lax.axis_index("col")
    layer_idx = lax.axis_index("layer")
    row_count = lax.axis_size("row")
    col_count = lax.axis_size("col")
    rows_local = left_matrix.shape[0]
    row_blocks = rows_local // BLK
    inner_blocks = left_matrix.shape[1] // BLK
    inner_local = square_term.shape[0]
    cols_local = square_term.shape[1]
    col_blocks = cols_local // BLK
    slots = (row_blocks // GROUP) * CAP
    total_inner_blocks = block_pattern.shape[1]

    inner_start = (layer_idx * col_count + col_idx) * inner_blocks
    pattern_patch = lax.dynamic_slice(
        block_pattern, (row_idx * row_blocks, inner_start), (row_blocks, inner_blocks)
    )
    stored, slot = slot_table(pattern_patch)
    slot_ids = jnp.arange(slots, dtype=jnp.int32)
    hit = (stored[:, :, None] > 0) & (slot[:, :, None] == slot_ids[None, None, :])
    source_row = jnp.sum(
        jnp.where(hit, jnp.arange(row_blocks, dtype=jnp.int32)[:, None, None], 0), axis=0
    )
    blocks = left_matrix.reshape(row_blocks, BLK, inner_blocks, BLK).transpose(2, 0, 1, 3)
    flat_blocks = blocks.reshape(inner_blocks * row_blocks, BLK, BLK)
    take_idx = source_row + (jnp.arange(inner_blocks, dtype=jnp.int32) * row_blocks)[:, None]
    packed = jnp.take(flat_blocks, take_idx.reshape(-1), axis=0)
    packed = packed.reshape(inner_blocks, slots, BLK, BLK)

    layer_count = lax.axis_size("layer")
    keep_patch = lax.dynamic_slice(
        keep_mask, (row_idx * row_blocks, col_idx * col_blocks), (row_blocks, col_blocks)
    ).astype(jnp.int32)
    panel_pattern = lax.dynamic_slice(
        block_pattern, (row_idx * row_blocks, 0), (row_blocks, total_inner_blocks)
    )

    first_inner = (layer_idx * row_count + row_idx) * inner_local
    first_col = col_idx * cols_local
    inner_pos = first_inner + lax.broadcasted_iota(jnp.int32, (inner_local, cols_local), 0)
    col_pos = first_col + lax.broadcasted_iota(jnp.int32, (inner_local, cols_local), 1)
    unit = jnp.where(inner_pos == col_pos, jnp.float32(1.5), jnp.float32(0.0))
    right_factor = (unit - 0.5 * square_term.astype(jnp.float32)).astype(jnp.bfloat16)

    use_permutes = (
        inner_blocks == 1
        and inner_local == BLK
        and col_count == row_count
        and col_count <= 4
        and layer_count <= 2
    )
    if use_permutes:
        own_over_layer = [
            lax.ppermute(packed[0], "layer", [(s, (s + m) % layer_count) for s in range(layer_count)])
            for m in range(1, layer_count)
        ]
        rf_pair, rf_layer_src = ring_gather(right_factor, "layer", layer_idx, layer_count)
        rf_pair = jnp.stack(rf_pair)
        col_pieces, piece_col = ring_gather(packed[0], "col", col_idx, col_count)
        pieces = [packed[0]] + own_over_layer
        for k in range(1, col_count):
            got, _ = ring_gather(col_pieces[k], "layer", layer_idx, layer_count)
            pieces.extend(got)
        piece_layer = [(layer_idx - m) % layer_count for k in range(col_count) for m in range(layer_count)]
        piece_col = [piece_col[k] for k in range(col_count) for m in range(layer_count)]
        piece_j = jnp.stack(
            [src_l * col_count + src_c for src_l, src_c in zip(piece_layer, piece_col)]
        ).astype(jnp.int32)
        rf_pieces, rf_row = ring_gather(rf_pair, "row", row_idx, row_count)
        rf_layer = [(layer_idx - m) % layer_count for k in range(row_count) for m in range(layer_count)]
        rf_row = [rf_row[k] for k in range(row_count) for m in range(layer_count)]
        rf_q = jnp.stack(
            [src_l * row_count + src_r for src_l, src_r in zip(rf_layer, rf_row)]
        ).astype(jnp.int32)
        rf_pos = ((col_idx - rf_q % col_count) % col_count) * layer_count + (
            (layer_idx - rf_q // col_count) % layer_count
        )
        p_stored, p_slot = slot_table(panel_pattern)
        slot_tbl = jnp.where(p_stored > 0, p_slot, -1)
        slot_tbl = jnp.take(slot_tbl, piece_j, axis=1).T.astype(jnp.int32)
        return product_call(slot_tbl, rf_pos.astype(jnp.int32), keep_patch, pieces, rf_pieces)

    gathered = lax.all_gather(packed, ("layer", "col"), axis=0, tiled=True)
    piece_j = jnp.arange(total_inner_blocks, dtype=jnp.int32)
    right_full = lax.all_gather(right_factor, ("layer", "row"), axis=0, tiled=True)

    p_stored, p_slot = slot_table(panel_pattern)
    p_stored = jnp.take(p_stored, piece_j, axis=1)
    p_slot = jnp.take(p_slot, piece_j, axis=1)
    gather_idx = (
        jnp.arange(total_inner_blocks, dtype=jnp.int32)[None, :] * slots
        + jnp.clip(p_slot, 0, slots - 1)
    )
    flat_packed = gathered.reshape(total_inner_blocks * slots, BLK, BLK)
    right_blocks = jnp.take(right_full.reshape(total_inner_blocks, BLK, cols_local), piece_j, axis=0)

    def chunk_sum(first, count):
        idx = lax.dynamic_slice_in_dim(gather_idx, first, count, axis=1)
        keep = lax.dynamic_slice_in_dim(p_stored, first, count, axis=1)
        dense = jnp.take(flat_packed, idx.reshape(-1), axis=0)
        dense = dense.reshape(row_blocks, count, BLK, BLK)
        dense = jnp.where(keep[:, :, None, None] > 0, dense, jnp.zeros_like(dense))
        rhs = lax.dynamic_slice_in_dim(right_blocks, first, count, axis=0)
        return jnp.einsum("ijab,jbc->iac", dense, rhs, preferred_element_type=jnp.float32)

    dense_bytes = row_blocks * total_inner_blocks * BLK * BLK * 2
    chunks = max(1, dense_bytes // (4 << 20))
    while total_inner_blocks % chunks:
        chunks += 1
    if chunks == 1:
        full_sum = chunk_sum(0, total_inner_blocks)
    else:
        per_chunk = total_inner_blocks // chunks

        def body(c, acc):
            return acc + chunk_sum(c * per_chunk, per_chunk)

        full_sum = lax.fori_loop(
            0, chunks, body, jnp.zeros((row_blocks, BLK, cols_local), jnp.float32)
        )
    full_sum = full_sum.reshape(rows_local, cols_local)

    keep_full = jnp.repeat(jnp.repeat(keep_patch, BLK, axis=0), BLK, axis=1)
    kept = jnp.where(keep_full > 0, full_sum, jnp.zeros_like(full_sum))
    return kept.astype(jnp.bfloat16)


def solution(mesh):
    return jax.shard_map(
        per_device,
        mesh=mesh,
        in_specs=(P("row", ("layer", "col")), P(("layer", "row"), "col"), P(), P()),
        out_specs=P("row", "col"),
        check_vma=False,
    )
```

```python
import functools

import jax
import jax.numpy as jnp
from jax import lax
from jax.experimental import pallas as pl
from jax.experimental.pallas import tpu as pltpu
from jax.sharding import PartitionSpec as P

BLK = 128
GROUP = 16
CAP = 8


def slot_table(pattern):
    stored = (pattern > 0).astype(jnp.int32)
    rows = pattern.shape[0]
    groups = rows // GROUP
    grouped = stored.reshape(groups, GROUP, -1)
    slot = jnp.cumsum(grouped, axis=1) - 1
    group_base = (jnp.arange(groups, dtype=jnp.int32) * CAP)[:, None, None]
    slot = (slot + group_base).reshape(rows, -1)
    return stored, slot


def ring_gather(x, axis, index, count):
    pieces = [x]
    for k in range(1, count):
        perm = [(s, (s + k) % count) for s in range(count)]
        pieces.append(lax.ppermute(x, axis, perm))
    sources = [(index - k) % count for k in range(count)]
    return pieces, sources


def ring_gather_list(xs, axis, index, count):
    out, sources = [], []
    for x in xs:
        got, src = ring_gather(x, axis, index, count)
        out.extend(got)
        sources.extend(src)
    return out, sources


def product_kernel(slot_ref, rf_pos_ref, keep_ref, *refs, pieces, rf_groups, row_blocks, cols):
    left_refs = refs[:pieces]
    rf_refs = refs[pieces:pieces + rf_groups]
    out_ref = refs[pieces + rf_groups]
    lhs_scr, rf_scr = refs[pieces + rf_groups + 1:]
    per_group = pieces // rf_groups
    for q in range(pieces):
        at = pl.multiple_of(rf_pos_ref[q] * BLK, BLK)
        rf_scr[pl.ds(at, BLK), :] = rf_refs[q // per_group][q % per_group]
    for p in range(pieces):
        for i in range(row_blocks):
            s = slot_ref[p, i]
            blk = left_refs[p][jnp.maximum(s, 0)]
            blk = jnp.where(s >= 0, blk, jnp.zeros_like(blk))
            lhs_scr[i * BLK:(i + 1) * BLK, p * BLK:(p + 1) * BLK] = blk
    tile = 2 * BLK
    for t in range(row_blocks * BLK // tile):
        res = jnp.dot(
            lhs_scr[t * tile:(t + 1) * tile, :], rf_scr[...], preferred_element_type=jnp.float32
        )
        for a in range(tile // BLK):
            i = t * (tile // BLK) + a
            for b in range(cols // BLK):
                sub = res[a * BLK:(a + 1) * BLK, b * BLK:(b + 1) * BLK]
                sub = jnp.where(keep_ref[i, b] > 0, sub, jnp.zeros_like(sub))
                out_ref[i * BLK:(i + 1) * BLK, b * BLK:(b + 1) * BLK] = sub.astype(out_ref.dtype)


def product_call(slot_tbl, rf_pos, keep_patch, left_pieces, rf_pieces):
    pieces = len(left_pieces)
    rf_groups = len(rf_pieces)
    row_blocks = slot_tbl.shape[1]
    cols = rf_pieces[0].shape[-1]
    smem = pl.BlockSpec(memory_space=pltpu.SMEM)
    vmem = pl.BlockSpec(memory_space=pltpu.VMEM)
    flops = 2 * row_blocks * BLK * pieces * BLK * cols
    bytes_accessed = (
        pieces * left_pieces[0].size * 2 + rf_groups * rf_pieces[0].size * 2 + row_blocks * BLK * cols * 2
    )
    return pl.pallas_call(
        functools.partial(
            product_kernel, pieces=pieces, rf_groups=rf_groups, row_blocks=row_blocks, cols=cols
        ),
        out_shape=jax.ShapeDtypeStruct((row_blocks * BLK, cols), jnp.bfloat16),
        in_specs=[smem, smem, smem] + [vmem] * (pieces + rf_groups),
        out_specs=vmem,
        scratch_shapes=[
            pltpu.VMEM((row_blocks * BLK, pieces * BLK), jnp.bfloat16),
            pltpu.VMEM((pieces * BLK, cols), jnp.bfloat16),
        ],
        cost_estimate=pl.CostEstimate(flops=flops, bytes_accessed=bytes_accessed, transcendentals=0),
    )(slot_tbl, rf_pos, keep_patch, *left_pieces, *rf_pieces)


def per_device(left_matrix, square_term, block_pattern, keep_mask):
    row_idx = lax.axis_index("row")
    col_idx = lax.axis_index("col")
    layer_idx = lax.axis_index("layer")
    row_count = lax.axis_size("row")
    col_count = lax.axis_size("col")
    rows_local = left_matrix.shape[0]
    row_blocks = rows_local // BLK
    inner_blocks = left_matrix.shape[1] // BLK
    inner_local = square_term.shape[0]
    cols_local = square_term.shape[1]
    col_blocks = cols_local // BLK
    slots = (row_blocks // GROUP) * CAP
    total_inner_blocks = block_pattern.shape[1]

    inner_start = (layer_idx * col_count + col_idx) * inner_blocks
    pattern_patch = lax.dynamic_slice(
        block_pattern, (row_idx * row_blocks, inner_start), (row_blocks, inner_blocks)
    )
    stored, slot = slot_table(pattern_patch)
    slot_ids = jnp.arange(slots, dtype=jnp.int32)
    hit = (stored[:, :, None] > 0) & (slot[:, :, None] == slot_ids[None, None, :])
    source_row = jnp.sum(
        jnp.where(hit, jnp.arange(row_blocks, dtype=jnp.int32)[:, None, None], 0), axis=0
    )
    blocks = left_matrix.reshape(row_blocks, BLK, inner_blocks, BLK).transpose(2, 0, 1, 3)
    flat_blocks = blocks.reshape(inner_blocks * row_blocks, BLK, BLK)
    take_idx = source_row + (jnp.arange(inner_blocks, dtype=jnp.int32) * row_blocks)[:, None]
    packed = jnp.take(flat_blocks, take_idx.reshape(-1), axis=0)
    packed = packed.reshape(inner_blocks, slots, BLK, BLK)

    layer_count = lax.axis_size("layer")
    keep_patch = lax.dynamic_slice(
        keep_mask, (row_idx * row_blocks, col_idx * col_blocks), (row_blocks, col_blocks)
    ).astype(jnp.int32)
    panel_pattern = lax.dynamic_slice(
        block_pattern, (row_idx * row_blocks, 0), (row_blocks, total_inner_blocks)
    )

    first_inner = (layer_idx * row_count + row_idx) * inner_local
    first_col = col_idx * cols_local
    inner_pos = first_inner + lax.broadcasted_iota(jnp.int32, (inner_local, cols_local), 0)
    col_pos = first_col + lax.broadcasted_iota(jnp.int32, (inner_local, cols_local), 1)
    unit = jnp.where(inner_pos == col_pos, jnp.float32(1.5), jnp.float32(0.0))
    right_factor = (unit - 0.5 * square_term.astype(jnp.float32)).astype(jnp.bfloat16)

    use_permutes = (
        inner_blocks == 1
        and inner_local == BLK
        and col_count == row_count
        and col_count <= 4
        and layer_count <= 2
    )
    if use_permutes:
        rf_pair, rf_layer_src = ring_gather(right_factor, "layer", layer_idx, layer_count)
        rf_pair = jnp.stack(rf_pair)
        own_over_layer = [
            lax.ppermute(packed[0], "layer", [(s, (s + m) % layer_count) for s in range(layer_count)])
            for m in range(1, layer_count)
        ]
        def col_shift(x, k):
            return lax.ppermute(x, "col", [(s, (s + k) % col_count) for s in range(col_count)])

        col_pieces = {1: col_shift(packed[0], 1)}
        later, col_pieces[1] = lax.optimization_barrier((packed[0], col_pieces[1]))
        for k in range(2, col_count):
            col_pieces[k] = col_shift(later, k)
        piece_col = [(col_idx - k) % col_count for k in range(col_count)]
        pieces = [packed[0]] + own_over_layer
        for k in range(1, col_count):
            got, _ = ring_gather(col_pieces[k], "layer", layer_idx, layer_count)
            pieces.extend(got)
        piece_layer = [(layer_idx - m) % layer_count for k in range(col_count) for m in range(layer_count)]
        piece_col = [piece_col[k] for k in range(col_count) for m in range(layer_count)]
        piece_j = jnp.stack(
            [src_l * col_count + src_c for src_l, src_c in zip(piece_layer, piece_col)]
        ).astype(jnp.int32)
        rf_pieces, rf_row = ring_gather(rf_pair, "row", row_idx, row_count)
        rf_layer = [(layer_idx - m) % layer_count for k in range(row_count) for m in range(layer_count)]
        rf_row = [rf_row[k] for k in range(row_count) for m in range(layer_count)]
        rf_q = jnp.stack(
            [src_l * row_count + src_r for src_l, src_r in zip(rf_layer, rf_row)]
        ).astype(jnp.int32)
        rf_pos = ((col_idx - rf_q % col_count) % col_count) * layer_count + (
            (layer_idx - rf_q // col_count) % layer_count
        )
        p_stored, p_slot = slot_table(panel_pattern)
        slot_tbl = jnp.where(p_stored > 0, p_slot, -1)
        slot_tbl = jnp.take(slot_tbl, piece_j, axis=1).T.astype(jnp.int32)
        return product_call(slot_tbl, rf_pos.astype(jnp.int32), keep_patch, pieces, rf_pieces)

    gathered = lax.all_gather(packed, ("layer", "col"), axis=0, tiled=True)
    piece_j = jnp.arange(total_inner_blocks, dtype=jnp.int32)
    right_full = lax.all_gather(right_factor, ("layer", "row"), axis=0, tiled=True)

    p_stored, p_slot = slot_table(panel_pattern)
    p_stored = jnp.take(p_stored, piece_j, axis=1)
    p_slot = jnp.take(p_slot, piece_j, axis=1)
    gather_idx = (
        jnp.arange(total_inner_blocks, dtype=jnp.int32)[None, :] * slots
        + jnp.clip(p_slot, 0, slots - 1)
    )
    flat_packed = gathered.reshape(total_inner_blocks * slots, BLK, BLK)
    right_blocks = jnp.take(right_full.reshape(total_inner_blocks, BLK, cols_local), piece_j, axis=0)

    def chunk_sum(first, count):
        idx = lax.dynamic_slice_in_dim(gather_idx, first, count, axis=1)
        keep = lax.dynamic_slice_in_dim(p_stored, first, count, axis=1)
        dense = jnp.take(flat_packed, idx.reshape(-1), axis=0)
        dense = dense.reshape(row_blocks, count, BLK, BLK)
        dense = jnp.where(keep[:, :, None, None] > 0, dense, jnp.zeros_like(dense))
        rhs = lax.dynamic_slice_in_dim(right_blocks, first, count, axis=0)
        return jnp.einsum("ijab,jbc->iac", dense, rhs, preferred_element_type=jnp.float32)

    dense_bytes = row_blocks * total_inner_blocks * BLK * BLK * 2
    chunks = max(1, dense_bytes // (4 << 20))
    while total_inner_blocks % chunks:
        chunks += 1
    if chunks == 1:
        full_sum = chunk_sum(0, total_inner_blocks)
    else:
        per_chunk = total_inner_blocks // chunks

        def body(c, acc):
            return acc + chunk_sum(c * per_chunk, per_chunk)

        full_sum = lax.fori_loop(
            0, chunks, body, jnp.zeros((row_blocks, BLK, cols_local), jnp.float32)
        )
    full_sum = full_sum.reshape(rows_local, cols_local)

    keep_full = jnp.repeat(jnp.repeat(keep_patch, BLK, axis=0), BLK, axis=1)
    kept = jnp.where(keep_full > 0, full_sum, jnp.zeros_like(full_sum))
    return kept.astype(jnp.bfloat16)


def solution(mesh):
    return jax.shard_map(
        per_device,
        mesh=mesh,
        in_specs=(P("row", ("layer", "col")), P(("layer", "row"), "col"), P(), P()),
        out_specs=P("row", "col"),
        check_vma=False,
    )
```

```python
import functools

import jax
import jax.numpy as jnp
from jax import lax
from jax.experimental import pallas as pl
from jax.experimental.pallas import tpu as pltpu
from jax.sharding import PartitionSpec as P

BLK = 128
GROUP = 16
CAP = 8


def slot_table(pattern):
    stored = (pattern > 0).astype(jnp.int32)
    rows = pattern.shape[0]
    groups = rows // GROUP
    grouped = stored.reshape(groups, GROUP, -1)
    slot = jnp.cumsum(grouped, axis=1) - 1
    group_base = (jnp.arange(groups, dtype=jnp.int32) * CAP)[:, None, None]
    slot = (slot + group_base).reshape(rows, -1)
    return stored, slot


def ring_gather(x, axis, index, count):
    pieces = [x]
    for k in range(1, count):
        perm = [(s, (s + k) % count) for s in range(count)]
        pieces.append(lax.ppermute(x, axis, perm))
    sources = [(index - k) % count for k in range(count)]
    return pieces, sources


def ring_gather_list(xs, axis, index, count):
    out, sources = [], []
    for x in xs:
        got, src = ring_gather(x, axis, index, count)
        out.extend(got)
        sources.extend(src)
    return out, sources


def product_kernel(slot_ref, rf_src_ref, keep_ref, rf_ref, *refs, pieces, row_blocks, with_acc, final):
    left_refs = refs[:pieces]
    at = pieces
    acc_ref = None
    if with_acc:
        acc_ref = refs[at]
        at += 1
    out_ref = refs[at]
    lhs_scr, rf_scr = refs[at + 1:]
    cols = rf_ref.shape[-1]
    for p in range(pieces):
        rf_scr[p * BLK:(p + 1) * BLK, :] = rf_ref[rf_src_ref[p]]
    for p in range(pieces):
        for i in range(row_blocks):
            s = slot_ref[p, i]
            blk = left_refs[p][jnp.maximum(s, 0)]
            blk = jnp.where(s >= 0, blk, jnp.zeros_like(blk))
            lhs_scr[i * BLK:(i + 1) * BLK, p * BLK:(p + 1) * BLK] = blk
    tile = 2 * BLK
    for t in range(row_blocks * BLK // tile):
        rows = slice(t * tile, (t + 1) * tile)
        res = jnp.dot(lhs_scr[rows, :], rf_scr[...], preferred_element_type=jnp.float32)
        if with_acc:
            res = res + acc_ref[rows, :]
        if not final:
            out_ref[rows, :] = res
            continue
        for a in range(tile // BLK):
            i = t * (tile // BLK) + a
            for b in range(cols // BLK):
                sub = res[a * BLK:(a + 1) * BLK, b * BLK:(b + 1) * BLK]
                sub = jnp.where(keep_ref[i, b] > 0, sub, jnp.zeros_like(sub))
                out_ref[i * BLK:(i + 1) * BLK, b * BLK:(b + 1) * BLK] = sub.astype(out_ref.dtype)


def product_call(slot_tbl, rf_src, keep_patch, rf_all, left_pieces, acc=None, final=True):
    pieces = len(left_pieces)
    row_blocks = slot_tbl.shape[1]
    cols = rf_all.shape[-1]
    smem = pl.BlockSpec(memory_space=pltpu.SMEM)
    vmem = pl.BlockSpec(memory_space=pltpu.VMEM)
    operands = [slot_tbl, rf_src, keep_patch, rf_all, *left_pieces]
    if acc is not None:
        operands.append(acc)
    out_dtype = jnp.bfloat16 if final else jnp.float32
    flops = 2 * row_blocks * BLK * pieces * BLK * cols
    bytes_accessed = (
        pieces * (left_pieces[0].size + BLK * cols) * 2
        + row_blocks * BLK * cols * (2 if final else 4)
        + (0 if acc is None else acc.size * 4)
    )
    return pl.pallas_call(
        functools.partial(
            product_kernel,
            pieces=pieces,
            row_blocks=row_blocks,
            with_acc=acc is not None,
            final=final,
        ),
        out_shape=jax.ShapeDtypeStruct((row_blocks * BLK, cols), out_dtype),
        in_specs=[smem, smem, smem] + [vmem] * (len(operands) - 3),
        out_specs=vmem,
        scratch_shapes=[
            pltpu.VMEM((row_blocks * BLK, pieces * BLK), jnp.bfloat16),
            pltpu.VMEM((pieces * BLK, cols), jnp.bfloat16),
        ],
        cost_estimate=pl.CostEstimate(flops=flops, bytes_accessed=bytes_accessed, transcendentals=0),
    )(*operands)


def per_device(left_matrix, square_term, block_pattern, keep_mask):
    row_idx = lax.axis_index("row")
    col_idx = lax.axis_index("col")
    layer_idx = lax.axis_index("layer")
    row_count = lax.axis_size("row")
    col_count = lax.axis_size("col")
    rows_local = left_matrix.shape[0]
    row_blocks = rows_local // BLK
    inner_blocks = left_matrix.shape[1] // BLK
    inner_local = square_term.shape[0]
    cols_local = square_term.shape[1]
    col_blocks = cols_local // BLK
    slots = (row_blocks // GROUP) * CAP
    total_inner_blocks = block_pattern.shape[1]

    inner_start = (layer_idx * col_count + col_idx) * inner_blocks
    pattern_patch = lax.dynamic_slice(
        block_pattern, (row_idx * row_blocks, inner_start), (row_blocks, inner_blocks)
    )
    stored, slot = slot_table(pattern_patch)
    slot_ids = jnp.arange(slots, dtype=jnp.int32)
    hit = (stored[:, :, None] > 0) & (slot[:, :, None] == slot_ids[None, None, :])
    source_row = jnp.sum(
        jnp.where(hit, jnp.arange(row_blocks, dtype=jnp.int32)[:, None, None], 0), axis=0
    )
    blocks = left_matrix.reshape(row_blocks, BLK, inner_blocks, BLK).transpose(2, 0, 1, 3)
    flat_blocks = blocks.reshape(inner_blocks * row_blocks, BLK, BLK)
    take_idx = source_row + (jnp.arange(inner_blocks, dtype=jnp.int32) * row_blocks)[:, None]
    packed = jnp.take(flat_blocks, take_idx.reshape(-1), axis=0)
    packed = packed.reshape(inner_blocks, slots, BLK, BLK)

    layer_count = lax.axis_size("layer")
    keep_patch = lax.dynamic_slice(
        keep_mask, (row_idx * row_blocks, col_idx * col_blocks), (row_blocks, col_blocks)
    ).astype(jnp.int32)
    panel_pattern = lax.dynamic_slice(
        block_pattern, (row_idx * row_blocks, 0), (row_blocks, total_inner_blocks)
    )

    first_inner = (layer_idx * row_count + row_idx) * inner_local
    first_col = col_idx * cols_local
    inner_pos = first_inner + lax.broadcasted_iota(jnp.int32, (inner_local, cols_local), 0)
    col_pos = first_col + lax.broadcasted_iota(jnp.int32, (inner_local, cols_local), 1)
    unit = jnp.where(inner_pos == col_pos, jnp.float32(1.5), jnp.float32(0.0))
    right_factor = (unit - 0.5 * square_term.astype(jnp.float32)).astype(jnp.bfloat16)

    use_permutes = (
        inner_blocks == 1
        and inner_local == BLK
        and col_count == row_count
        and col_count <= 4
        and layer_count <= 2
    )
    if use_permutes:
        rf_pair, _ = ring_gather(right_factor, "layer", layer_idx, layer_count)
        rf_pair = jnp.stack(rf_pair)
        own_over_layer = [
            lax.ppermute(packed[0], "layer", [(s, (s + m) % layer_count) for s in range(layer_count)])
            for m in range(1, layer_count)
        ]

        def col_shift(x, k):
            return lax.ppermute(x, "col", [(s, (s + k) % col_count) for s in range(col_count)])

        col_pieces = {1: col_shift(packed[0], 1)}
        rf_pieces, _ = ring_gather(rf_pair, "row", row_idx, row_count)
        rf_all = jnp.concatenate(rf_pieces, axis=0)
        later, col_pieces[1], rf_all = lax.optimization_barrier((packed[0], col_pieces[1], rf_all))
        for k in range(2, col_count):
            col_pieces[k] = col_shift(later, k)
        pieces = [packed[0]] + own_over_layer
        for k in range(1, col_count):
            got, _ = ring_gather(col_pieces[k], "layer", layer_idx, layer_count)
            pieces.extend(got)
        piece_layer = [(layer_idx - m) % layer_count for k in range(col_count) for m in range(layer_count)]
        piece_col = [(col_idx - k) % col_count for k in range(col_count) for m in range(layer_count)]
        piece_j = jnp.stack(
            [src_l * col_count + src_c for src_l, src_c in zip(piece_layer, piece_col)]
        ).astype(jnp.int32)
        rf_src = ((row_idx - piece_j % row_count) % row_count) * layer_count + (
            (layer_idx - piece_j // row_count) % layer_count
        )
        rf_src = rf_src.astype(jnp.int32)
        p_stored, p_slot = slot_table(panel_pattern)
        slot_tbl = jnp.where(p_stored > 0, p_slot, -1)
        slot_tbl = jnp.take(slot_tbl, piece_j, axis=1).T.astype(jnp.int32)
        last = [k * layer_count + m for k in range(2, col_count) for m in range(1, layer_count)]
        first = [p for p in range(len(pieces)) if p not in last]
        partial = product_call(
            slot_tbl[jnp.array(first)], rf_src[jnp.array(first)], keep_patch, rf_all,
            [pieces[p] for p in first], final=False,
        )
        return product_call(
            slot_tbl[jnp.array(last)], rf_src[jnp.array(last)], keep_patch, rf_all,
            [pieces[p] for p in last], acc=partial, final=True,
        )

    gathered = lax.all_gather(packed, ("layer", "col"), axis=0, tiled=True)
    piece_j = jnp.arange(total_inner_blocks, dtype=jnp.int32)
    right_full = lax.all_gather(right_factor, ("layer", "row"), axis=0, tiled=True)

    p_stored, p_slot = slot_table(panel_pattern)
    p_stored = jnp.take(p_stored, piece_j, axis=1)
    p_slot = jnp.take(p_slot, piece_j, axis=1)
    gather_idx = (
        jnp.arange(total_inner_blocks, dtype=jnp.int32)[None, :] * slots
        + jnp.clip(p_slot, 0, slots - 1)
    )
    flat_packed = gathered.reshape(total_inner_blocks * slots, BLK, BLK)
    right_blocks = jnp.take(right_full.reshape(total_inner_blocks, BLK, cols_local), piece_j, axis=0)

    def chunk_sum(first, count):
        idx = lax.dynamic_slice_in_dim(gather_idx, first, count, axis=1)
        keep = lax.dynamic_slice_in_dim(p_stored, first, count, axis=1)
        dense = jnp.take(flat_packed, idx.reshape(-1), axis=0)
        dense = dense.reshape(row_blocks, count, BLK, BLK)
        dense = jnp.where(keep[:, :, None, None] > 0, dense, jnp.zeros_like(dense))
        rhs = lax.dynamic_slice_in_dim(right_blocks, first, count, axis=0)
        return jnp.einsum("ijab,jbc->iac", dense, rhs, preferred_element_type=jnp.float32)

    dense_bytes = row_blocks * total_inner_blocks * BLK * BLK * 2
    chunks = max(1, dense_bytes // (4 << 20))
    while total_inner_blocks % chunks:
        chunks += 1
    if chunks == 1:
        full_sum = chunk_sum(0, total_inner_blocks)
    else:
        per_chunk = total_inner_blocks // chunks

        def body(c, acc):
            return acc + chunk_sum(c * per_chunk, per_chunk)

        full_sum = lax.fori_loop(
            0, chunks, body, jnp.zeros((row_blocks, BLK, cols_local), jnp.float32)
        )
    full_sum = full_sum.reshape(rows_local, cols_local)

    keep_full = jnp.repeat(jnp.repeat(keep_patch, BLK, axis=0), BLK, axis=1)
    kept = jnp.where(keep_full > 0, full_sum, jnp.zeros_like(full_sum))
    return kept.astype(jnp.bfloat16)


def solution(mesh):
    return jax.shard_map(
        per_device,
        mesh=mesh,
        in_specs=(P("row", ("layer", "col")), P(("layer", "row"), "col"), P(), P()),
        out_specs=P("row", "col"),
        check_vma=False,
    )
```

```python
import functools

import jax
import jax.numpy as jnp
from jax import lax
from jax.experimental import pallas as pl
from jax.experimental.pallas import tpu as pltpu
from jax.sharding import PartitionSpec as P

BLK = 128
GROUP = 16
CAP = 8


def slot_table(pattern):
    stored = (pattern > 0).astype(jnp.int32)
    rows = pattern.shape[0]
    groups = rows // GROUP
    grouped = stored.reshape(groups, GROUP, -1)
    slot = jnp.cumsum(grouped, axis=1) - 1
    group_base = (jnp.arange(groups, dtype=jnp.int32) * CAP)[:, None, None]
    slot = (slot + group_base).reshape(rows, -1)
    return stored, slot


def ring_gather(x, axis, index, count):
    pieces = [x]
    for k in range(1, count):
        perm = [(s, (s + k) % count) for s in range(count)]
        pieces.append(lax.ppermute(x, axis, perm))
    sources = [(index - k) % count for k in range(count)]
    return pieces, sources


def ring_gather_list(xs, axis, index, count):
    out, sources = [], []
    for x in xs:
        got, src = ring_gather(x, axis, index, count)
        out.extend(got)
        sources.extend(src)
    return out, sources


def product_kernel(slot_ref, rf_src_ref, keep_ref, rf_ref, *refs, pieces, row_blocks, with_acc, final):
    left_refs = refs[:pieces]
    at = pieces
    acc_ref = None
    if with_acc:
        acc_ref = refs[at]
        at += 1
    out_ref = refs[at]
    lhs_scr, rf_scr = refs[at + 1:]
    cols = rf_ref.shape[-1]
    for p in range(pieces):
        rf_scr[p * BLK:(p + 1) * BLK, :] = rf_ref[rf_src_ref[p]]
    for p in range(pieces):
        for i in range(row_blocks):
            s = slot_ref[p, i]
            blk = left_refs[p][jnp.maximum(s, 0)]
            blk = jnp.where(s >= 0, blk, jnp.zeros_like(blk))
            lhs_scr[i * BLK:(i + 1) * BLK, p * BLK:(p + 1) * BLK] = blk
    tile = 2 * BLK
    for t in range(row_blocks * BLK // tile):
        rows = slice(t * tile, (t + 1) * tile)
        res = jnp.dot(lhs_scr[rows, :], rf_scr[...], preferred_element_type=jnp.float32)
        if with_acc:
            res = res + acc_ref[rows, :]
        if not final:
            out_ref[rows, :] = res
            continue
        for a in range(tile // BLK):
            i = t * (tile // BLK) + a
            for b in range(cols // BLK):
                sub = res[a * BLK:(a + 1) * BLK, b * BLK:(b + 1) * BLK]
                sub = jnp.where(keep_ref[i, b] > 0, sub, jnp.zeros_like(sub))
                out_ref[i * BLK:(i + 1) * BLK, b * BLK:(b + 1) * BLK] = sub.astype(out_ref.dtype)


def product_call(slot_tbl, rf_src, keep_patch, rf_all, left_pieces, acc=None, final=True):
    pieces = len(left_pieces)
    row_blocks = slot_tbl.shape[1]
    cols = rf_all.shape[-1]
    smem = pl.BlockSpec(memory_space=pltpu.SMEM)
    vmem = pl.BlockSpec(memory_space=pltpu.VMEM)
    operands = [slot_tbl, rf_src, keep_patch, rf_all, *left_pieces]
    if acc is not None:
        operands.append(acc)
    out_dtype = jnp.bfloat16 if final else jnp.float32
    flops = 2 * row_blocks * BLK * pieces * BLK * cols
    bytes_accessed = (
        pieces * (left_pieces[0].size + BLK * cols) * 2
        + row_blocks * BLK * cols * (2 if final else 4)
        + (0 if acc is None else acc.size * 4)
    )
    return pl.pallas_call(
        functools.partial(
            product_kernel,
            pieces=pieces,
            row_blocks=row_blocks,
            with_acc=acc is not None,
            final=final,
        ),
        out_shape=jax.ShapeDtypeStruct((row_blocks * BLK, cols), out_dtype),
        in_specs=[smem, smem, smem] + [vmem] * (len(operands) - 3),
        out_specs=vmem,
        scratch_shapes=[
            pltpu.VMEM((row_blocks * BLK, pieces * BLK), jnp.bfloat16),
            pltpu.VMEM((pieces * BLK, cols), jnp.bfloat16),
        ],
        cost_estimate=pl.CostEstimate(flops=flops, bytes_accessed=bytes_accessed, transcendentals=0),
    )(*operands)


def per_device(left_matrix, square_term, block_pattern, keep_mask):
    row_idx = lax.axis_index("row")
    col_idx = lax.axis_index("col")
    layer_idx = lax.axis_index("layer")
    row_count = lax.axis_size("row")
    col_count = lax.axis_size("col")
    rows_local = left_matrix.shape[0]
    row_blocks = rows_local // BLK
    inner_blocks = left_matrix.shape[1] // BLK
    inner_local = square_term.shape[0]
    cols_local = square_term.shape[1]
    col_blocks = cols_local // BLK
    slots = (row_blocks // GROUP) * CAP
    total_inner_blocks = block_pattern.shape[1]

    inner_start = (layer_idx * col_count + col_idx) * inner_blocks
    pattern_patch = lax.dynamic_slice(
        block_pattern, (row_idx * row_blocks, inner_start), (row_blocks, inner_blocks)
    )
    stored, slot = slot_table(pattern_patch)
    slot_ids = jnp.arange(slots, dtype=jnp.int32)
    hit = (stored[:, :, None] > 0) & (slot[:, :, None] == slot_ids[None, None, :])
    source_row = jnp.sum(
        jnp.where(hit, jnp.arange(row_blocks, dtype=jnp.int32)[:, None, None], 0), axis=0
    )
    blocks = left_matrix.reshape(row_blocks, BLK, inner_blocks, BLK).transpose(2, 0, 1, 3)
    flat_blocks = blocks.reshape(inner_blocks * row_blocks, BLK, BLK)
    take_idx = source_row + (jnp.arange(inner_blocks, dtype=jnp.int32) * row_blocks)[:, None]
    packed = jnp.take(flat_blocks, take_idx.reshape(-1), axis=0)
    packed = packed.reshape(inner_blocks, slots, BLK, BLK)

    layer_count = lax.axis_size("layer")
    keep_patch = lax.dynamic_slice(
        keep_mask, (row_idx * row_blocks, col_idx * col_blocks), (row_blocks, col_blocks)
    ).astype(jnp.int32)
    panel_pattern = lax.dynamic_slice(
        block_pattern, (row_idx * row_blocks, 0), (row_blocks, total_inner_blocks)
    )

    first_inner = (layer_idx * row_count + row_idx) * inner_local
    first_col = col_idx * cols_local
    inner_pos = first_inner + lax.broadcasted_iota(jnp.int32, (inner_local, cols_local), 0)
    col_pos = first_col + lax.broadcasted_iota(jnp.int32, (inner_local, cols_local), 1)
    unit = jnp.where(inner_pos == col_pos, jnp.float32(1.5), jnp.float32(0.0))
    right_factor = (unit - 0.5 * square_term.astype(jnp.float32)).astype(jnp.bfloat16)

    use_permutes = (
        inner_blocks == 1
        and inner_local == BLK
        and col_count == 4
        and row_count == 4
        and layer_count == 2
        and cols_local % BLK == 0
    )
    if use_permutes:
        rf_blocks = right_factor.reshape(BLK, cols_local // BLK, BLK).transpose(1, 0, 2)
        own_plus = jnp.concatenate([packed[0], rf_blocks], axis=0)
        other_plus = lax.ppermute(own_plus, "layer", [(0, 1), (1, 0)])
        other_rf = other_plus[slots:].transpose(1, 0, 2).reshape(BLK, cols_local)

        def col_shift(x, k):
            return lax.ppermute(x, "col", [(s, (s + k) % col_count) for s in range(col_count)])

        col_pieces = {1: col_shift(packed[0], 1)}
        later, col_pieces[1] = lax.optimization_barrier((packed[0], col_pieces[1]))
        for k in range(2, col_count):
            col_pieces[k] = col_shift(later, k)
        pieces = [packed[0], other_plus]
        for k in range(1, col_count):
            pieces.append(col_pieces[k])
            pieces.append(lax.ppermute(col_pieces[k], "layer", [(0, 1), (1, 0)]))
        piece_layer = [layer_idx ^ m for k in range(col_count) for m in range(2)]
        piece_col = [(col_idx - k) % col_count for k in range(col_count) for m in range(2)]
        piece_j = jnp.stack(
            [src_l * col_count + src_c for src_l, src_c in zip(piece_layer, piece_col)]
        ).astype(jnp.int32)
        rf_pair = jnp.stack([right_factor, other_rf])
        rf_quad = jnp.concatenate(
            [rf_pair, lax.ppermute(rf_pair, "row", [(s, s ^ 1) for s in range(4)])], axis=0
        )
        rf_all = jnp.concatenate(
            [rf_quad, lax.ppermute(rf_quad, "row", [(s, s ^ 2) for s in range(4)])], axis=0
        )
        src_row = piece_j % row_count
        src_layer = piece_j // row_count
        rf_src = (
            (((row_idx ^ src_row) >> 1) & 1) * 4 + ((row_idx ^ src_row) & 1) * 2 + (layer_idx ^ src_layer)
        ).astype(jnp.int32)
        p_stored, p_slot = slot_table(panel_pattern)
        slot_tbl = jnp.where(p_stored > 0, p_slot, -1)
        slot_tbl = jnp.take(slot_tbl, piece_j, axis=1).T.astype(jnp.int32)
        return product_call(slot_tbl, rf_src, keep_patch, rf_all, pieces)

    gathered = lax.all_gather(packed, ("layer", "col"), axis=0, tiled=True)
    piece_j = jnp.arange(total_inner_blocks, dtype=jnp.int32)
    right_full = lax.all_gather(right_factor, ("layer", "row"), axis=0, tiled=True)

    p_stored, p_slot = slot_table(panel_pattern)
    p_stored = jnp.take(p_stored, piece_j, axis=1)
    p_slot = jnp.take(p_slot, piece_j, axis=1)
    gather_idx = (
        jnp.arange(total_inner_blocks, dtype=jnp.int32)[None, :] * slots
        + jnp.clip(p_slot, 0, slots - 1)
    )
    flat_packed = gathered.reshape(total_inner_blocks * slots, BLK, BLK)
    right_blocks = jnp.take(right_full.reshape(total_inner_blocks, BLK, cols_local), piece_j, axis=0)

    def chunk_sum(first, count):
        idx = lax.dynamic_slice_in_dim(gather_idx, first, count, axis=1)
        keep = lax.dynamic_slice_in_dim(p_stored, first, count, axis=1)
        dense = jnp.take(flat_packed, idx.reshape(-1), axis=0)
        dense = dense.reshape(row_blocks, count, BLK, BLK)
        dense = jnp.where(keep[:, :, None, None] > 0, dense, jnp.zeros_like(dense))
        rhs = lax.dynamic_slice_in_dim(right_blocks, first, count, axis=0)
        return jnp.einsum("ijab,jbc->iac", dense, rhs, preferred_element_type=jnp.float32)

    dense_bytes = row_blocks * total_inner_blocks * BLK * BLK * 2
    chunks = max(1, dense_bytes // (4 << 20))
    while total_inner_blocks % chunks:
        chunks += 1
    if chunks == 1:
        full_sum = chunk_sum(0, total_inner_blocks)
    else:
        per_chunk = total_inner_blocks // chunks

        def body(c, acc):
            return acc + chunk_sum(c * per_chunk, per_chunk)

        full_sum = lax.fori_loop(
            0, chunks, body, jnp.zeros((row_blocks, BLK, cols_local), jnp.float32)
        )
    full_sum = full_sum.reshape(rows_local, cols_local)

    keep_full = jnp.repeat(jnp.repeat(keep_patch, BLK, axis=0), BLK, axis=1)
    kept = jnp.where(keep_full > 0, full_sum, jnp.zeros_like(full_sum))
    return kept.astype(jnp.bfloat16)


def solution(mesh):
    return jax.shard_map(
        per_device,
        mesh=mesh,
        in_specs=(P("row", ("layer", "col")), P(("layer", "row"), "col"), P(), P()),
        out_specs=P("row", "col"),
        check_vma=False,
    )
```

```python
import functools

import jax
import jax.numpy as jnp
from jax import lax
from jax.experimental import pallas as pl
from jax.experimental.pallas import tpu as pltpu
from jax.sharding import PartitionSpec as P

BLK = 128
GROUP = 16
CAP = 8


def slot_table(pattern):
    stored = (pattern > 0).astype(jnp.int32)
    rows = pattern.shape[0]
    groups = rows // GROUP
    grouped = stored.reshape(groups, GROUP, -1)
    slot = jnp.cumsum(grouped, axis=1) - 1
    group_base = (jnp.arange(groups, dtype=jnp.int32) * CAP)[:, None, None]
    slot = (slot + group_base).reshape(rows, -1)
    return stored, slot


def ring_gather(x, axis, index, count):
    pieces = [x]
    for k in range(1, count):
        perm = [(s, (s + k) % count) for s in range(count)]
        pieces.append(lax.ppermute(x, axis, perm))
    sources = [(index - k) % count for k in range(count)]
    return pieces, sources


def ring_gather_list(xs, axis, index, count):
    out, sources = [], []
    for x in xs:
        got, src = ring_gather(x, axis, index, count)
        out.extend(got)
        sources.extend(src)
    return out, sources


def product_kernel(slot_ref, rf_src_ref, keep_ref, rf_ref, *refs, parts, n_left, row_blocks):
    left_refs = refs[:n_left]
    out_ref = refs[n_left]
    lhs_scr, rf_scr = refs[n_left + 1:]
    cols = rf_ref.shape[-1]
    pieces = len(parts)
    for p in range(pieces):
        rf_scr[p * BLK:(p + 1) * BLK, :] = rf_ref[rf_src_ref[p]]
    for p in range(pieces):
        for i in range(row_blocks):
            s = slot_ref[p, i]
            blk = jnp.zeros((BLK, BLK), lhs_scr.dtype)
            for ref_id, first, count, offset in parts[p]:
                cand = left_refs[ref_id][offset + jnp.clip(s - first, 0, count - 1)]
                blk = jnp.where((s >= first) & (s < first + count), cand, blk)
            lhs_scr[i * BLK:(i + 1) * BLK, p * BLK:(p + 1) * BLK] = blk
    tile = 2 * BLK
    for t in range(row_blocks * BLK // tile):
        rows = slice(t * tile, (t + 1) * tile)
        res = jnp.dot(lhs_scr[rows, :], rf_scr[...], preferred_element_type=jnp.float32)
        for a in range(tile // BLK):
            i = t * (tile // BLK) + a
            for b in range(cols // BLK):
                sub = res[a * BLK:(a + 1) * BLK, b * BLK:(b + 1) * BLK]
                sub = jnp.where(keep_ref[i, b] > 0, sub, jnp.zeros_like(sub))
                out_ref[i * BLK:(i + 1) * BLK, b * BLK:(b + 1) * BLK] = sub.astype(out_ref.dtype)


def product_call(slot_tbl, rf_src, keep_patch, rf_all, piece_operands):
    row_blocks = slot_tbl.shape[1]
    cols = rf_all.shape[-1]
    parts, flat, ids = [], [], {}
    for spans in piece_operands:
        first, pp = 0, []
        for op, offset, count in spans:
            if id(op) not in ids:
                ids[id(op)] = len(flat)
                flat.append(op)
            pp.append((ids[id(op)], first, count, offset))
            first += count
        parts.append(tuple(pp))
    pieces = len(parts)
    smem = pl.BlockSpec(memory_space=pltpu.SMEM)
    vmem = pl.BlockSpec(memory_space=pltpu.VMEM)
    flops = 2 * row_blocks * BLK * pieces * BLK * cols
    bytes_accessed = sum(op.size for op in flat) * 2 + pieces * BLK * cols * 2 + row_blocks * BLK * cols * 2
    return pl.pallas_call(
        functools.partial(product_kernel, parts=tuple(parts), n_left=len(flat), row_blocks=row_blocks),
        out_shape=jax.ShapeDtypeStruct((row_blocks * BLK, cols), jnp.bfloat16),
        in_specs=[smem, smem, smem, vmem] + [vmem] * len(flat),
        out_specs=vmem,
        scratch_shapes=[
            pltpu.VMEM((row_blocks * BLK, pieces * BLK), jnp.bfloat16),
            pltpu.VMEM((pieces * BLK, cols), jnp.bfloat16),
        ],
        cost_estimate=pl.CostEstimate(flops=flops, bytes_accessed=bytes_accessed, transcendentals=0),
    )(slot_tbl, rf_src, keep_patch, rf_all, *flat)


def per_device(left_matrix, square_term, block_pattern, keep_mask):
    row_idx = lax.axis_index("row")
    col_idx = lax.axis_index("col")
    layer_idx = lax.axis_index("layer")
    row_count = lax.axis_size("row")
    col_count = lax.axis_size("col")
    rows_local = left_matrix.shape[0]
    row_blocks = rows_local // BLK
    inner_blocks = left_matrix.shape[1] // BLK
    inner_local = square_term.shape[0]
    cols_local = square_term.shape[1]
    col_blocks = cols_local // BLK
    slots = (row_blocks // GROUP) * CAP
    total_inner_blocks = block_pattern.shape[1]

    inner_start = (layer_idx * col_count + col_idx) * inner_blocks
    pattern_patch = lax.dynamic_slice(
        block_pattern, (row_idx * row_blocks, inner_start), (row_blocks, inner_blocks)
    )
    stored, slot = slot_table(pattern_patch)
    slot_ids = jnp.arange(slots, dtype=jnp.int32)
    hit = (stored[:, :, None] > 0) & (slot[:, :, None] == slot_ids[None, None, :])
    source_row = jnp.sum(
        jnp.where(hit, jnp.arange(row_blocks, dtype=jnp.int32)[:, None, None], 0), axis=0
    )
    blocks = left_matrix.reshape(row_blocks, BLK, inner_blocks, BLK).transpose(2, 0, 1, 3)
    flat_blocks = blocks.reshape(inner_blocks * row_blocks, BLK, BLK)
    take_idx = source_row + (jnp.arange(inner_blocks, dtype=jnp.int32) * row_blocks)[:, None]
    packed = jnp.take(flat_blocks, take_idx.reshape(-1), axis=0)
    packed = packed.reshape(inner_blocks, slots, BLK, BLK)

    layer_count = lax.axis_size("layer")
    keep_patch = lax.dynamic_slice(
        keep_mask, (row_idx * row_blocks, col_idx * col_blocks), (row_blocks, col_blocks)
    ).astype(jnp.int32)
    panel_pattern = lax.dynamic_slice(
        block_pattern, (row_idx * row_blocks, 0), (row_blocks, total_inner_blocks)
    )

    first_inner = (layer_idx * row_count + row_idx) * inner_local
    first_col = col_idx * cols_local
    inner_pos = first_inner + lax.broadcasted_iota(jnp.int32, (inner_local, cols_local), 0)
    col_pos = first_col + lax.broadcasted_iota(jnp.int32, (inner_local, cols_local), 1)
    unit = jnp.where(inner_pos == col_pos, jnp.float32(1.5), jnp.float32(0.0))
    right_factor = (unit - 0.5 * square_term.astype(jnp.float32)).astype(jnp.bfloat16)

    use_permutes = (
        inner_blocks == 1
        and inner_local == BLK
        and col_count == 4
        and row_count == 4
        and layer_count == 2
        and cols_local % BLK == 0
    )
    if use_permutes:
        rf_row_pieces, _ = ring_gather(right_factor, "row", row_idx, row_count)
        rf_own = jnp.stack(rf_row_pieces)
        swap = [(0, 1), (1, 0)]
        own_over_layer = lax.ppermute(packed[0], "layer", swap)
        rf_all = jnp.concatenate([rf_own, lax.ppermute(rf_own, "layer", swap)], axis=0)

        def col_shift(x, k):
            return lax.ppermute(x, "col", [(s, (s + k) % col_count) for s in range(col_count)])

        half = slots // 2
        s1 = col_shift(packed[0], 1)
        s2a = col_shift(packed[0][:half], 2)
        later, s1, s2a, own_over_layer, rf_all = lax.optimization_barrier(
            (packed[0], s1, s2a, own_over_layer, rf_all)
        )
        s3 = col_shift(later, 3)
        s2b = col_shift(later[half:], 2)
        fwd1 = lax.ppermute(jnp.concatenate([s1, s2a], axis=0), "layer", swap)
        fwd2 = lax.ppermute(jnp.concatenate([s3, s2b], axis=0), "layer", swap)
        piece_ops = [
            [(packed[0], 0, slots)],
            [(own_over_layer, 0, slots)],
            [(s1, 0, slots)],
            [(fwd1, 0, slots)],
            [(s2a, 0, half), (s2b, 0, slots - half)],
            [(fwd1, slots, half), (fwd2, slots, slots - half)],
            [(s3, 0, slots)],
            [(fwd2, 0, slots)],
        ]
        piece_layer = [layer_idx ^ m for k in range(col_count) for m in range(2)]
        piece_col = [(col_idx - k) % col_count for k in range(col_count) for m in range(2)]
        piece_j = jnp.stack(
            [src_l * col_count + src_c for src_l, src_c in zip(piece_layer, piece_col)]
        ).astype(jnp.int32)
        rf_src = (layer_idx ^ (piece_j // row_count)) * row_count + (
            (row_idx - piece_j % row_count) % row_count
        )
        rf_src = rf_src.astype(jnp.int32)
        p_stored, p_slot = slot_table(panel_pattern)
        slot_tbl = jnp.where(p_stored > 0, p_slot, -1)
        slot_tbl = jnp.take(slot_tbl, piece_j, axis=1).T.astype(jnp.int32)
        return product_call(slot_tbl, rf_src, keep_patch, rf_all, piece_ops)

    gathered = lax.all_gather(packed, ("layer", "col"), axis=0, tiled=True)
    piece_j = jnp.arange(total_inner_blocks, dtype=jnp.int32)
    right_full = lax.all_gather(right_factor, ("layer", "row"), axis=0, tiled=True)

    p_stored, p_slot = slot_table(panel_pattern)
    p_stored = jnp.take(p_stored, piece_j, axis=1)
    p_slot = jnp.take(p_slot, piece_j, axis=1)
    gather_idx = (
        jnp.arange(total_inner_blocks, dtype=jnp.int32)[None, :] * slots
        + jnp.clip(p_slot, 0, slots - 1)
    )
    flat_packed = gathered.reshape(total_inner_blocks * slots, BLK, BLK)
    right_blocks = jnp.take(right_full.reshape(total_inner_blocks, BLK, cols_local), piece_j, axis=0)

    def chunk_sum(first, count):
        idx = lax.dynamic_slice_in_dim(gather_idx, first, count, axis=1)
        keep = lax.dynamic_slice_in_dim(p_stored, first, count, axis=1)
        dense = jnp.take(flat_packed, idx.reshape(-1), axis=0)
        dense = dense.reshape(row_blocks, count, BLK, BLK)
        dense = jnp.where(keep[:, :, None, None] > 0, dense, jnp.zeros_like(dense))
        rhs = lax.dynamic_slice_in_dim(right_blocks, first, count, axis=0)
        return jnp.einsum("ijab,jbc->iac", dense, rhs, preferred_element_type=jnp.float32)

    dense_bytes = row_blocks * total_inner_blocks * BLK * BLK * 2
    chunks = max(1, dense_bytes // (4 << 20))
    while total_inner_blocks % chunks:
        chunks += 1
    if chunks == 1:
        full_sum = chunk_sum(0, total_inner_blocks)
    else:
        per_chunk = total_inner_blocks // chunks

        def body(c, acc):
            return acc + chunk_sum(c * per_chunk, per_chunk)

        full_sum = lax.fori_loop(
            0, chunks, body, jnp.zeros((row_blocks, BLK, cols_local), jnp.float32)
        )
    full_sum = full_sum.reshape(rows_local, cols_local)

    keep_full = jnp.repeat(jnp.repeat(keep_patch, BLK, axis=0), BLK, axis=1)
    kept = jnp.where(keep_full > 0, full_sum, jnp.zeros_like(full_sum))
    return kept.astype(jnp.bfloat16)


def solution(mesh):
    return jax.shard_map(
        per_device,
        mesh=mesh,
        in_specs=(P("row", ("layer", "col")), P(("layer", "row"), "col"), P(), P()),
        out_specs=P("row", "col"),
        check_vma=False,
    )
```

```python
import functools

import jax
import jax.numpy as jnp
from jax import lax
from jax.experimental import pallas as pl
from jax.experimental.pallas import tpu as pltpu
from jax.sharding import PartitionSpec as P

BLK = 128
GROUP = 16
CAP = 8


def slot_table(pattern):
    stored = (pattern > 0).astype(jnp.int32)
    rows = pattern.shape[0]
    groups = rows // GROUP
    grouped = stored.reshape(groups, GROUP, -1)
    slot = jnp.cumsum(grouped, axis=1) - 1
    group_base = (jnp.arange(groups, dtype=jnp.int32) * CAP)[:, None, None]
    slot = (slot + group_base).reshape(rows, -1)
    return stored, slot


def ring_gather(x, axis, index, count):
    pieces = [x]
    for k in range(1, count):
        perm = [(s, (s + k) % count) for s in range(count)]
        pieces.append(lax.ppermute(x, axis, perm))
    sources = [(index - k) % count for k in range(count)]
    return pieces, sources


def ring_gather_list(xs, axis, index, count):
    out, sources = [], []
    for x in xs:
        got, src = ring_gather(x, axis, index, count)
        out.extend(got)
        sources.extend(src)
    return out, sources


def product_kernel(slot_ref, rf_src_ref, keep_ref, rf_ref, *refs, parts, n_left, row_blocks):
    left_refs = refs[:n_left]
    out_ref = refs[n_left]
    lhs_scr, rf_scr = refs[n_left + 1:]
    cols = rf_ref.shape[-1]
    pieces = len(parts)
    for p in range(pieces):
        rf_scr[p * BLK:(p + 1) * BLK, :] = rf_ref[rf_src_ref[p]]
    for p in range(pieces):
        for i in range(row_blocks):
            s = slot_ref[p, i]
            blk = jnp.zeros((BLK, BLK), lhs_scr.dtype)
            for ref_id, first, count, offset in parts[p]:
                cand = left_refs[ref_id][offset + jnp.clip(s - first, 0, count - 1)]
                blk = jnp.where((s >= first) & (s < first + count), cand, blk)
            lhs_scr[i * BLK:(i + 1) * BLK, p * BLK:(p + 1) * BLK] = blk
    tile = 2 * BLK
    for t in range(row_blocks * BLK // tile):
        rows = slice(t * tile, (t + 1) * tile)
        res = jnp.dot(lhs_scr[rows, :], rf_scr[...], preferred_element_type=jnp.float32)
        for a in range(tile // BLK):
            i = t * (tile // BLK) + a
            for b in range(cols // BLK):
                sub = res[a * BLK:(a + 1) * BLK, b * BLK:(b + 1) * BLK]
                sub = jnp.where(keep_ref[i, b] > 0, sub, jnp.zeros_like(sub))
                out_ref[i * BLK:(i + 1) * BLK, b * BLK:(b + 1) * BLK] = sub.astype(out_ref.dtype)


def product_call(slot_tbl, rf_src, keep_patch, rf_all, piece_operands):
    row_blocks = slot_tbl.shape[1]
    cols = rf_all.shape[-1]
    parts, flat, ids = [], [], {}
    for spans in piece_operands:
        first, pp = 0, []
        for op, offset, count in spans:
            if id(op) not in ids:
                ids[id(op)] = len(flat)
                flat.append(op)
            pp.append((ids[id(op)], first, count, offset))
            first += count
        parts.append(tuple(pp))
    pieces = len(parts)
    smem = pl.BlockSpec(memory_space=pltpu.SMEM)
    vmem = pl.BlockSpec(memory_space=pltpu.VMEM)
    flops = 2 * row_blocks * BLK * pieces * BLK * cols
    bytes_accessed = sum(op.size for op in flat) * 2 + pieces * BLK * cols * 2 + row_blocks * BLK * cols * 2
    return pl.pallas_call(
        functools.partial(product_kernel, parts=tuple(parts), n_left=len(flat), row_blocks=row_blocks),
        out_shape=jax.ShapeDtypeStruct((row_blocks * BLK, cols), jnp.bfloat16),
        in_specs=[smem, smem, smem, vmem] + [vmem] * len(flat),
        out_specs=vmem,
        scratch_shapes=[
            pltpu.VMEM((row_blocks * BLK, pieces * BLK), jnp.bfloat16),
            pltpu.VMEM((pieces * BLK, cols), jnp.bfloat16),
        ],
        cost_estimate=pl.CostEstimate(flops=flops, bytes_accessed=bytes_accessed, transcendentals=0),
    )(slot_tbl, rf_src, keep_patch, rf_all, *flat)


def per_device(left_matrix, square_term, block_pattern, keep_mask):
    row_idx = lax.axis_index("row")
    col_idx = lax.axis_index("col")
    layer_idx = lax.axis_index("layer")
    row_count = lax.axis_size("row")
    col_count = lax.axis_size("col")
    rows_local = left_matrix.shape[0]
    row_blocks = rows_local // BLK
    inner_blocks = left_matrix.shape[1] // BLK
    inner_local = square_term.shape[0]
    cols_local = square_term.shape[1]
    col_blocks = cols_local // BLK
    slots = (row_blocks // GROUP) * CAP
    total_inner_blocks = block_pattern.shape[1]

    inner_start = (layer_idx * col_count + col_idx) * inner_blocks
    pattern_patch = lax.dynamic_slice(
        block_pattern, (row_idx * row_blocks, inner_start), (row_blocks, inner_blocks)
    )
    stored, slot = slot_table(pattern_patch)
    slot_ids = jnp.arange(slots, dtype=jnp.int32)
    hit = (stored[:, :, None] > 0) & (slot[:, :, None] == slot_ids[None, None, :])
    source_row = jnp.sum(
        jnp.where(hit, jnp.arange(row_blocks, dtype=jnp.int32)[:, None, None], 0), axis=0
    )
    blocks = left_matrix.reshape(row_blocks, BLK, inner_blocks, BLK).transpose(2, 0, 1, 3)
    flat_blocks = blocks.reshape(inner_blocks * row_blocks, BLK, BLK)
    take_idx = source_row + (jnp.arange(inner_blocks, dtype=jnp.int32) * row_blocks)[:, None]
    packed = jnp.take(flat_blocks, take_idx.reshape(-1), axis=0)
    packed = packed.reshape(inner_blocks, slots, BLK, BLK)

    layer_count = lax.axis_size("layer")
    keep_patch = lax.dynamic_slice(
        keep_mask, (row_idx * row_blocks, col_idx * col_blocks), (row_blocks, col_blocks)
    ).astype(jnp.int32)
    panel_pattern = lax.dynamic_slice(
        block_pattern, (row_idx * row_blocks, 0), (row_blocks, total_inner_blocks)
    )

    first_inner = (layer_idx * row_count + row_idx) * inner_local
    first_col = col_idx * cols_local
    inner_pos = first_inner + lax.broadcasted_iota(jnp.int32, (inner_local, cols_local), 0)
    col_pos = first_col + lax.broadcasted_iota(jnp.int32, (inner_local, cols_local), 1)
    unit = jnp.where(inner_pos == col_pos, jnp.float32(1.5), jnp.float32(0.0))
    right_factor = (unit - 0.5 * square_term.astype(jnp.float32)).astype(jnp.bfloat16)

    use_permutes = (
        inner_blocks == 1
        and inner_local == BLK
        and col_count == 4
        and row_count == 4
        and layer_count == 2
        and cols_local % BLK == 0
    )
    if use_permutes:
        swap = [(0, 1), (1, 0)]
        own_over_layer = lax.ppermute(packed[0], "layer", swap)
        rf_pair = jnp.stack([right_factor, lax.ppermute(right_factor, "layer", swap)])

        piece_layer = [layer_idx ^ m for k in range(col_count) for m in range(2)]
        piece_col = [(col_idx - k) % col_count for k in range(col_count) for m in range(2)]
        piece_j = jnp.stack(
            [src_l * col_count + src_c for src_l, src_c in zip(piece_layer, piece_col)]
        ).astype(jnp.int32)
        rf_src = ((row_idx - piece_j % row_count) % row_count) * 2 + (layer_idx ^ (piece_j // row_count))
        rf_src = rf_src.astype(jnp.int32)
        p_stored, p_slot = slot_table(panel_pattern)
        slot_tbl = jnp.where(p_stored > 0, p_slot, -1)
        slot_tbl = jnp.take(slot_tbl, piece_j, axis=1).T.astype(jnp.int32)

        def col_shift(x, k):
            return lax.ppermute(x, "col", [(s, (s + k) % col_count) for s in range(col_count)])

        half = slots // 2
        s1 = col_shift(packed[0], 1)
        s2a = col_shift(packed[0][:half], 2)
        later, s1, s2a, own_over_layer, slot_tbl, rf_src, keep_patch = lax.optimization_barrier(
            (packed[0], s1, s2a, own_over_layer, slot_tbl, rf_src, keep_patch)
        )
        s3 = col_shift(later, 3)
        s2b = col_shift(later[half:], 2)
        fwd1 = lax.ppermute(jnp.concatenate([s1, s2a], axis=0), "layer", swap)
        rf_pair, fwd1 = lax.optimization_barrier((rf_pair, fwd1))
        rf_pieces, _ = ring_gather(rf_pair, "row", row_idx, row_count)
        rf_all = jnp.concatenate(rf_pieces, axis=0)
        fwd2 = lax.ppermute(jnp.concatenate([s3, s2b], axis=0), "layer", swap)
        piece_ops = [
            [(packed[0], 0, slots)],
            [(own_over_layer, 0, slots)],
            [(s1, 0, slots)],
            [(fwd1, 0, slots)],
            [(s2a, 0, half), (s2b, 0, slots - half)],
            [(fwd1, slots, half), (fwd2, slots, slots - half)],
            [(s3, 0, slots)],
            [(fwd2, 0, slots)],
        ]
        return product_call(slot_tbl, rf_src, keep_patch, rf_all, piece_ops)

    gathered = lax.all_gather(packed, ("layer", "col"), axis=0, tiled=True)
    piece_j = jnp.arange(total_inner_blocks, dtype=jnp.int32)
    right_full = lax.all_gather(right_factor, ("layer", "row"), axis=0, tiled=True)

    p_stored, p_slot = slot_table(panel_pattern)
    p_stored = jnp.take(p_stored, piece_j, axis=1)
    p_slot = jnp.take(p_slot, piece_j, axis=1)
    gather_idx = (
        jnp.arange(total_inner_blocks, dtype=jnp.int32)[None, :] * slots
        + jnp.clip(p_slot, 0, slots - 1)
    )
    flat_packed = gathered.reshape(total_inner_blocks * slots, BLK, BLK)
    right_blocks = jnp.take(right_full.reshape(total_inner_blocks, BLK, cols_local), piece_j, axis=0)

    def chunk_sum(first, count):
        idx = lax.dynamic_slice_in_dim(gather_idx, first, count, axis=1)
        keep = lax.dynamic_slice_in_dim(p_stored, first, count, axis=1)
        dense = jnp.take(flat_packed, idx.reshape(-1), axis=0)
        dense = dense.reshape(row_blocks, count, BLK, BLK)
        dense = jnp.where(keep[:, :, None, None] > 0, dense, jnp.zeros_like(dense))
        rhs = lax.dynamic_slice_in_dim(right_blocks, first, count, axis=0)
        return jnp.einsum("ijab,jbc->iac", dense, rhs, preferred_element_type=jnp.float32)

    dense_bytes = row_blocks * total_inner_blocks * BLK * BLK * 2
    chunks = max(1, dense_bytes // (4 << 20))
    while total_inner_blocks % chunks:
        chunks += 1
    if chunks == 1:
        full_sum = chunk_sum(0, total_inner_blocks)
    else:
        per_chunk = total_inner_blocks // chunks

        def body(c, acc):
            return acc + chunk_sum(c * per_chunk, per_chunk)

        full_sum = lax.fori_loop(
            0, chunks, body, jnp.zeros((row_blocks, BLK, cols_local), jnp.float32)
        )
    full_sum = full_sum.reshape(rows_local, cols_local)

    keep_full = jnp.repeat(jnp.repeat(keep_patch, BLK, axis=0), BLK, axis=1)
    kept = jnp.where(keep_full > 0, full_sum, jnp.zeros_like(full_sum))
    return kept.astype(jnp.bfloat16)


def solution(mesh):
    return jax.shard_map(
        per_device,
        mesh=mesh,
        in_specs=(P("row", ("layer", "col")), P(("layer", "row"), "col"), P(), P()),
        out_specs=P("row", "col"),
        check_vma=False,
    )
```

```python
import functools

import jax
import jax.numpy as jnp
from jax import lax
from jax.experimental import pallas as pl
from jax.experimental.pallas import tpu as pltpu
from jax.sharding import PartitionSpec as P

BLK = 128
GROUP = 16
CAP = 8


def slot_table(pattern):
    stored = (pattern > 0).astype(jnp.int32)
    rows = pattern.shape[0]
    groups = rows // GROUP
    grouped = stored.reshape(groups, GROUP, -1)
    slot = jnp.cumsum(grouped, axis=1) - 1
    group_base = (jnp.arange(groups, dtype=jnp.int32) * CAP)[:, None, None]
    slot = (slot + group_base).reshape(rows, -1)
    return stored, slot


def ring_gather(x, axis, index, count):
    pieces = [x]
    for k in range(1, count):
        perm = [(s, (s + k) % count) for s in range(count)]
        pieces.append(lax.ppermute(x, axis, perm))
    sources = [(index - k) % count for k in range(count)]
    return pieces, sources


def ring_gather_list(xs, axis, index, count):
    out, sources = [], []
    for x in xs:
        got, src = ring_gather(x, axis, index, count)
        out.extend(got)
        sources.extend(src)
    return out, sources


def product_kernel(slot_ref, rf_pos_ref, keep_ref, *refs, pieces, rf_groups, row_blocks, cols):
    left_refs = refs[:pieces]
    rf_refs = refs[pieces:pieces + rf_groups]
    out_ref = refs[pieces + rf_groups]
    lhs_scr, rf_scr = refs[pieces + rf_groups + 1:]
    per_group = pieces // rf_groups
    for q in range(pieces):
        at = pl.multiple_of(rf_pos_ref[q] * BLK, BLK)
        rf_scr[pl.ds(at, BLK), :] = rf_refs[q // per_group][q % per_group]
    for p in range(pieces):
        for i in range(row_blocks):
            s = slot_ref[p, i]
            blk = left_refs[p][jnp.maximum(s, 0)]
            blk = jnp.where(s >= 0, blk, jnp.zeros_like(blk))
            lhs_scr[i * BLK:(i + 1) * BLK, p * BLK:(p + 1) * BLK] = blk
    tile = 2 * BLK
    for t in range(row_blocks * BLK // tile):
        res = jnp.dot(
            lhs_scr[t * tile:(t + 1) * tile, :], rf_scr[...], preferred_element_type=jnp.float32
        )
        for a in range(tile // BLK):
            i = t * (tile // BLK) + a
            for b in range(cols // BLK):
                sub = res[a * BLK:(a + 1) * BLK, b * BLK:(b + 1) * BLK]
                sub = jnp.where(keep_ref[i, b] > 0, sub, jnp.zeros_like(sub))
                out_ref[i * BLK:(i + 1) * BLK, b * BLK:(b + 1) * BLK] = sub.astype(out_ref.dtype)


def product_call(slot_tbl, rf_pos, keep_patch, left_pieces, rf_pieces):
    pieces = len(left_pieces)
    rf_groups = len(rf_pieces)
    row_blocks = slot_tbl.shape[1]
    cols = rf_pieces[0].shape[-1]
    smem = pl.BlockSpec(memory_space=pltpu.SMEM)
    vmem = pl.BlockSpec(memory_space=pltpu.VMEM)
    flops = 2 * row_blocks * BLK * pieces * BLK * cols
    bytes_accessed = (
        pieces * left_pieces[0].size * 2 + rf_groups * rf_pieces[0].size * 2 + row_blocks * BLK * cols * 2
    )
    return pl.pallas_call(
        functools.partial(
            product_kernel, pieces=pieces, rf_groups=rf_groups, row_blocks=row_blocks, cols=cols
        ),
        out_shape=jax.ShapeDtypeStruct((row_blocks * BLK, cols), jnp.bfloat16),
        in_specs=[smem, smem, smem] + [vmem] * (pieces + rf_groups),
        out_specs=vmem,
        scratch_shapes=[
            pltpu.VMEM((row_blocks * BLK, pieces * BLK), jnp.bfloat16),
            pltpu.VMEM((pieces * BLK, cols), jnp.bfloat16),
        ],
        cost_estimate=pl.CostEstimate(flops=flops, bytes_accessed=bytes_accessed, transcendentals=0),
    )(slot_tbl, rf_pos, keep_patch, *left_pieces, *rf_pieces)


def per_device(left_matrix, square_term, block_pattern, keep_mask):
    row_idx = lax.axis_index("row")
    col_idx = lax.axis_index("col")
    layer_idx = lax.axis_index("layer")
    row_count = lax.axis_size("row")
    col_count = lax.axis_size("col")
    rows_local = left_matrix.shape[0]
    row_blocks = rows_local // BLK
    inner_blocks = left_matrix.shape[1] // BLK
    inner_local = square_term.shape[0]
    cols_local = square_term.shape[1]
    col_blocks = cols_local // BLK
    slots = (row_blocks // GROUP) * CAP
    total_inner_blocks = block_pattern.shape[1]

    inner_start = (layer_idx * col_count + col_idx) * inner_blocks
    pattern_patch = lax.dynamic_slice(
        block_pattern, (row_idx * row_blocks, inner_start), (row_blocks, inner_blocks)
    )
    stored, slot = slot_table(pattern_patch)
    slot_ids = jnp.arange(slots, dtype=jnp.int32)
    hit = (stored[:, :, None] > 0) & (slot[:, :, None] == slot_ids[None, None, :])
    source_row = jnp.sum(
        jnp.where(hit, jnp.arange(row_blocks, dtype=jnp.int32)[:, None, None], 0), axis=0
    )
    blocks = left_matrix.reshape(row_blocks, BLK, inner_blocks, BLK).transpose(2, 0, 1, 3)
    flat_blocks = blocks.reshape(inner_blocks * row_blocks, BLK, BLK)
    take_idx = source_row + (jnp.arange(inner_blocks, dtype=jnp.int32) * row_blocks)[:, None]
    packed = jnp.take(flat_blocks, take_idx.reshape(-1), axis=0)
    packed = packed.reshape(inner_blocks, slots, BLK, BLK)

    layer_count = lax.axis_size("layer")
    keep_patch = lax.dynamic_slice(
        keep_mask, (row_idx * row_blocks, col_idx * col_blocks), (row_blocks, col_blocks)
    ).astype(jnp.int32)
    panel_pattern = lax.dynamic_slice(
        block_pattern, (row_idx * row_blocks, 0), (row_blocks, total_inner_blocks)
    )

    first_inner = (layer_idx * row_count + row_idx) * inner_local
    first_col = col_idx * cols_local
    inner_pos = first_inner + lax.broadcasted_iota(jnp.int32, (inner_local, cols_local), 0)
    col_pos = first_col + lax.broadcasted_iota(jnp.int32, (inner_local, cols_local), 1)
    unit = jnp.where(inner_pos == col_pos, jnp.float32(1.5), jnp.float32(0.0))
    right_factor = (unit - 0.5 * square_term.astype(jnp.float32)).astype(jnp.bfloat16)

    use_permutes = (
        inner_blocks == 1
        and inner_local == BLK
        and col_count == row_count
        and col_count <= 4
        and layer_count <= 2
    )
    if use_permutes:
        rf_pair, rf_layer_src = ring_gather(right_factor, "layer", layer_idx, layer_count)
        rf_pair = jnp.stack(rf_pair)
        own_over_layer = [
            lax.ppermute(packed[0], "layer", [(s, (s + m) % layer_count) for s in range(layer_count)])
            for m in range(1, layer_count)
        ]
        def col_shift(x, k):
            return lax.ppermute(x, "col", [(s, (s + k) % col_count) for s in range(col_count)])

        col_pieces = {1: col_shift(packed[0], 1)}
        piece_layer = [(layer_idx - m) % layer_count for k in range(col_count) for m in range(layer_count)]
        piece_src_col = [(col_idx - k) % col_count for k in range(col_count) for m in range(layer_count)]
        piece_j = jnp.stack(
            [src_l * col_count + src_c for src_l, src_c in zip(piece_layer, piece_src_col)]
        ).astype(jnp.int32)
        rf_row = [(row_idx - k) % row_count for k in range(row_count) for m in range(layer_count)]
        rf_layer = [(layer_idx - m) % layer_count for k in range(row_count) for m in range(layer_count)]
        rf_q = jnp.stack([src_l * row_count + src_r for src_l, src_r in zip(rf_layer, rf_row)])
        rf_pos = ((col_idx - rf_q % col_count) % col_count) * layer_count + (
            (layer_idx - rf_q // col_count) % layer_count
        )
        p_stored, p_slot = slot_table(panel_pattern)
        slot_tbl = jnp.where(p_stored > 0, p_slot, -1).astype(jnp.int32)
        slot_tbl = jnp.take(slot_tbl, piece_j, axis=1).T
        later, col_pieces[1], slot_tbl, rf_pos, keep_patch, own_over_layer = lax.optimization_barrier(
            (packed[0], col_pieces[1], slot_tbl, rf_pos.astype(jnp.int32), keep_patch, own_over_layer)
        )
        for k in range(2, col_count):
            col_pieces[k] = col_shift(later, k)
        piece_col = [(col_idx - k) % col_count for k in range(col_count)]
        pieces = [packed[0]] + own_over_layer
        for k in range(1, col_count):
            got, _ = ring_gather(col_pieces[k], "layer", layer_idx, layer_count)
            pieces.extend(got)
        rf_pieces, _ = ring_gather(rf_pair, "row", row_idx, row_count)
        return product_call(slot_tbl, rf_pos, keep_patch, pieces, rf_pieces)

    gathered = lax.all_gather(packed, ("layer", "col"), axis=0, tiled=True)
    piece_j = jnp.arange(total_inner_blocks, dtype=jnp.int32)
    right_full = lax.all_gather(right_factor, ("layer", "row"), axis=0, tiled=True)

    p_stored, p_slot = slot_table(panel_pattern)
    p_stored = jnp.take(p_stored, piece_j, axis=1)
    p_slot = jnp.take(p_slot, piece_j, axis=1)
    gather_idx = (
        jnp.arange(total_inner_blocks, dtype=jnp.int32)[None, :] * slots
        + jnp.clip(p_slot, 0, slots - 1)
    )
    flat_packed = gathered.reshape(total_inner_blocks * slots, BLK, BLK)
    right_blocks = jnp.take(right_full.reshape(total_inner_blocks, BLK, cols_local), piece_j, axis=0)

    def chunk_sum(first, count):
        idx = lax.dynamic_slice_in_dim(gather_idx, first, count, axis=1)
        keep = lax.dynamic_slice_in_dim(p_stored, first, count, axis=1)
        dense = jnp.take(flat_packed, idx.reshape(-1), axis=0)
        dense = dense.reshape(row_blocks, count, BLK, BLK)
        dense = jnp.where(keep[:, :, None, None] > 0, dense, jnp.zeros_like(dense))
        rhs = lax.dynamic_slice_in_dim(right_blocks, first, count, axis=0)
        return jnp.einsum("ijab,jbc->iac", dense, rhs, preferred_element_type=jnp.float32)

    dense_bytes = row_blocks * total_inner_blocks * BLK * BLK * 2
    chunks = max(1, dense_bytes // (4 << 20))
    while total_inner_blocks % chunks:
        chunks += 1
    if chunks == 1:
        full_sum = chunk_sum(0, total_inner_blocks)
    else:
        per_chunk = total_inner_blocks // chunks

        def body(c, acc):
            return acc + chunk_sum(c * per_chunk, per_chunk)

        full_sum = lax.fori_loop(
            0, chunks, body, jnp.zeros((row_blocks, BLK, cols_local), jnp.float32)
        )
    full_sum = full_sum.reshape(rows_local, cols_local)

    keep_full = jnp.repeat(jnp.repeat(keep_patch, BLK, axis=0), BLK, axis=1)
    kept = jnp.where(keep_full > 0, full_sum, jnp.zeros_like(full_sum))
    return kept.astype(jnp.bfloat16)


def solution(mesh):
    return jax.shard_map(
        per_device,
        mesh=mesh,
        in_specs=(P("row", ("layer", "col")), P(("layer", "row"), "col"), P(), P()),
        out_specs=P("row", "col"),
        check_vma=False,
    )
```

```python
import functools

import jax
import jax.numpy as jnp
from jax import lax
from jax.experimental import pallas as pl
from jax.experimental.pallas import tpu as pltpu
from jax.sharding import PartitionSpec as P

BLK = 128
GROUP = 16
CAP = 8


def slot_table(pattern):
    stored = (pattern > 0).astype(jnp.int32)
    rows = pattern.shape[0]
    groups = rows // GROUP
    grouped = stored.reshape(groups, GROUP, -1)
    slot = jnp.cumsum(grouped, axis=1) - 1
    group_base = (jnp.arange(groups, dtype=jnp.int32) * CAP)[:, None, None]
    slot = (slot + group_base).reshape(rows, -1)
    return stored, slot


def ring_gather(x, axis, index, count):
    pieces = [x]
    for k in range(1, count):
        perm = [(s, (s + k) % count) for s in range(count)]
        pieces.append(lax.ppermute(x, axis, perm))
    sources = [(index - k) % count for k in range(count)]
    return pieces, sources


def ring_gather_list(xs, axis, index, count):
    out, sources = [], []
    for x in xs:
        got, src = ring_gather(x, axis, index, count)
        out.extend(got)
        sources.extend(src)
    return out, sources


def product_kernel(slot_ref, rf_pos_ref, keep_ref, *refs, pieces, rf_groups, row_blocks, cols):
    left_refs = refs[:pieces]
    rf_refs = refs[pieces:pieces + rf_groups]
    out_ref = refs[pieces + rf_groups]
    lhs_scr, rf_scr = refs[pieces + rf_groups + 1:]
    per_group = pieces // rf_groups
    for q in range(pieces):
        at = pl.multiple_of(rf_pos_ref[q] * BLK, BLK)
        rf_scr[pl.ds(at, BLK), :] = rf_refs[q // per_group][q % per_group]
    for p in range(pieces):
        for i in range(row_blocks):
            s = slot_ref[p, i]
            blk = left_refs[p][jnp.maximum(s, 0)]
            blk = jnp.where(s >= 0, blk, jnp.zeros_like(blk))
            lhs_scr[i * BLK:(i + 1) * BLK, p * BLK:(p + 1) * BLK] = blk
    tile = 4 * BLK
    for t in range(row_blocks * BLK // tile):
        res = jnp.dot(
            lhs_scr[t * tile:(t + 1) * tile, :], rf_scr[...], preferred_element_type=jnp.float32
        )
        for a in range(tile // BLK):
            i = t * (tile // BLK) + a
            for b in range(cols // BLK):
                sub = res[a * BLK:(a + 1) * BLK, b * BLK:(b + 1) * BLK]
                sub = jnp.where(keep_ref[i, b] > 0, sub, jnp.zeros_like(sub))
                out_ref[i * BLK:(i + 1) * BLK, b * BLK:(b + 1) * BLK] = sub.astype(out_ref.dtype)


def product_call(slot_tbl, rf_pos, keep_patch, left_pieces, rf_pieces):
    pieces = len(left_pieces)
    rf_groups = len(rf_pieces)
    row_blocks = slot_tbl.shape[1]
    cols = rf_pieces[0].shape[-1]
    smem = pl.BlockSpec(memory_space=pltpu.SMEM)
    vmem = pl.BlockSpec(memory_space=pltpu.VMEM)
    flops = 2 * row_blocks * BLK * pieces * BLK * cols
    bytes_accessed = (
        pieces * left_pieces[0].size * 2 + rf_groups * rf_pieces[0].size * 2 + row_blocks * BLK * cols * 2
    )
    return pl.pallas_call(
        functools.partial(
            product_kernel, pieces=pieces, rf_groups=rf_groups, row_blocks=row_blocks, cols=cols
        ),
        out_shape=jax.ShapeDtypeStruct((row_blocks * BLK, cols), jnp.bfloat16),
        in_specs=[smem, smem, smem] + [vmem] * (pieces + rf_groups),
        out_specs=vmem,
        scratch_shapes=[
            pltpu.VMEM((row_blocks * BLK, pieces * BLK), jnp.bfloat16),
            pltpu.VMEM((pieces * BLK, cols), jnp.bfloat16),
        ],
        cost_estimate=pl.CostEstimate(flops=flops, bytes_accessed=bytes_accessed, transcendentals=0),
    )(slot_tbl, rf_pos, keep_patch, *left_pieces, *rf_pieces)


def per_device(left_matrix, square_term, block_pattern, keep_mask):
    row_idx = lax.axis_index("row")
    col_idx = lax.axis_index("col")
    layer_idx = lax.axis_index("layer")
    row_count = lax.axis_size("row")
    col_count = lax.axis_size("col")
    rows_local = left_matrix.shape[0]
    row_blocks = rows_local // BLK
    inner_blocks = left_matrix.shape[1] // BLK
    inner_local = square_term.shape[0]
    cols_local = square_term.shape[1]
    col_blocks = cols_local // BLK
    slots = (row_blocks // GROUP) * CAP
    total_inner_blocks = block_pattern.shape[1]

    inner_start = (layer_idx * col_count + col_idx) * inner_blocks
    pattern_patch = lax.dynamic_slice(
        block_pattern, (row_idx * row_blocks, inner_start), (row_blocks, inner_blocks)
    )
    stored, slot = slot_table(pattern_patch)
    slot_ids = jnp.arange(slots, dtype=jnp.int32)
    hit = (stored[:, :, None] > 0) & (slot[:, :, None] == slot_ids[None, None, :])
    source_row = jnp.sum(
        jnp.where(hit, jnp.arange(row_blocks, dtype=jnp.int32)[:, None, None], 0), axis=0
    )
    blocks = left_matrix.reshape(row_blocks, BLK, inner_blocks, BLK).transpose(2, 0, 1, 3)
    flat_blocks = blocks.reshape(inner_blocks * row_blocks, BLK, BLK)
    take_idx = source_row + (jnp.arange(inner_blocks, dtype=jnp.int32) * row_blocks)[:, None]
    packed = jnp.take(flat_blocks, take_idx.reshape(-1), axis=0)
    packed = packed.reshape(inner_blocks, slots, BLK, BLK)

    layer_count = lax.axis_size("layer")
    keep_patch = lax.dynamic_slice(
        keep_mask, (row_idx * row_blocks, col_idx * col_blocks), (row_blocks, col_blocks)
    ).astype(jnp.int32)
    panel_pattern = lax.dynamic_slice(
        block_pattern, (row_idx * row_blocks, 0), (row_blocks, total_inner_blocks)
    )

    first_inner = (layer_idx * row_count + row_idx) * inner_local
    first_col = col_idx * cols_local
    inner_pos = first_inner + lax.broadcasted_iota(jnp.int32, (inner_local, cols_local), 0)
    col_pos = first_col + lax.broadcasted_iota(jnp.int32, (inner_local, cols_local), 1)
    unit = jnp.where(inner_pos == col_pos, jnp.float32(1.5), jnp.float32(0.0))
    right_factor = (unit - 0.5 * square_term.astype(jnp.float32)).astype(jnp.bfloat16)

    use_permutes = (
        inner_blocks == 1
        and inner_local == BLK
        and col_count == row_count
        and col_count <= 4
        and layer_count <= 2
    )
    if use_permutes:
        rf_pair, rf_layer_src = ring_gather(right_factor, "layer", layer_idx, layer_count)
        rf_pair = jnp.stack(rf_pair)
        own_over_layer = [
            lax.ppermute(packed[0], "layer", [(s, (s + m) % layer_count) for s in range(layer_count)])
            for m in range(1, layer_count)
        ]
        def col_shift(x, k):
            return lax.ppermute(x, "col", [(s, (s + k) % col_count) for s in range(col_count)])

        col_pieces = {1: col_shift(packed[0], 1)}
        piece_layer = [(layer_idx - m) % layer_count for k in range(col_count) for m in range(layer_count)]
        piece_src_col = [(col_idx - k) % col_count for k in range(col_count) for m in range(layer_count)]
        piece_j = jnp.stack(
            [src_l * col_count + src_c for src_l, src_c in zip(piece_layer, piece_src_col)]
        ).astype(jnp.int32)
        rf_row = [(row_idx - k) % row_count for k in range(row_count) for m in range(layer_count)]
        rf_layer = [(layer_idx - m) % layer_count for k in range(row_count) for m in range(layer_count)]
        rf_q = jnp.stack([src_l * row_count + src_r for src_l, src_r in zip(rf_layer, rf_row)])
        rf_pos = ((col_idx - rf_q % col_count) % col_count) * layer_count + (
            (layer_idx - rf_q // col_count) % layer_count
        )
        p_stored, p_slot = slot_table(panel_pattern)
        slot_tbl = jnp.where(p_stored > 0, p_slot, -1).astype(jnp.int32)
        slot_tbl = jnp.take(slot_tbl, piece_j, axis=1).T
        later, col_pieces[1], slot_tbl, rf_pos, keep_patch, own_over_layer = lax.optimization_barrier(
            (packed[0], col_pieces[1], slot_tbl, rf_pos.astype(jnp.int32), keep_patch, own_over_layer)
        )
        for k in range(2, col_count):
            col_pieces[k] = col_shift(later, k)
        piece_col = [(col_idx - k) % col_count for k in range(col_count)]
        pieces = [packed[0]] + own_over_layer
        for k in range(1, col_count):
            got, _ = ring_gather(col_pieces[k], "layer", layer_idx, layer_count)
            pieces.extend(got)
        rf_pieces, _ = ring_gather(rf_pair, "row", row_idx, row_count)
        return product_call(slot_tbl, rf_pos, keep_patch, pieces, rf_pieces)

    gathered = lax.all_gather(packed, ("layer", "col"), axis=0, tiled=True)
    piece_j = jnp.arange(total_inner_blocks, dtype=jnp.int32)
    right_full = lax.all_gather(right_factor, ("layer", "row"), axis=0, tiled=True)

    p_stored, p_slot = slot_table(panel_pattern)
    p_stored = jnp.take(p_stored, piece_j, axis=1)
    p_slot = jnp.take(p_slot, piece_j, axis=1)
    gather_idx = (
        jnp.arange(total_inner_blocks, dtype=jnp.int32)[None, :] * slots
        + jnp.clip(p_slot, 0, slots - 1)
    )
    flat_packed = gathered.reshape(total_inner_blocks * slots, BLK, BLK)
    right_blocks = jnp.take(right_full.reshape(total_inner_blocks, BLK, cols_local), piece_j, axis=0)

    def chunk_sum(first, count):
        idx = lax.dynamic_slice_in_dim(gather_idx, first, count, axis=1)
        keep = lax.dynamic_slice_in_dim(p_stored, first, count, axis=1)
        dense = jnp.take(flat_packed, idx.reshape(-1), axis=0)
        dense = dense.reshape(row_blocks, count, BLK, BLK)
        dense = jnp.where(keep[:, :, None, None] > 0, dense, jnp.zeros_like(dense))
        rhs = lax.dynamic_slice_in_dim(right_blocks, first, count, axis=0)
        return jnp.einsum("ijab,jbc->iac", dense, rhs, preferred_element_type=jnp.float32)

    dense_bytes = row_blocks * total_inner_blocks * BLK * BLK * 2
    chunks = max(1, dense_bytes // (4 << 20))
    while total_inner_blocks % chunks:
        chunks += 1
    if chunks == 1:
        full_sum = chunk_sum(0, total_inner_blocks)
    else:
        per_chunk = total_inner_blocks // chunks

        def body(c, acc):
            return acc + chunk_sum(c * per_chunk, per_chunk)

        full_sum = lax.fori_loop(
            0, chunks, body, jnp.zeros((row_blocks, BLK, cols_local), jnp.float32)
        )
    full_sum = full_sum.reshape(rows_local, cols_local)

    keep_full = jnp.repeat(jnp.repeat(keep_patch, BLK, axis=0), BLK, axis=1)
    kept = jnp.where(keep_full > 0, full_sum, jnp.zeros_like(full_sum))
    return kept.astype(jnp.bfloat16)


def solution(mesh):
    return jax.shard_map(
        per_device,
        mesh=mesh,
        in_specs=(P("row", ("layer", "col")), P(("layer", "row"), "col"), P(), P()),
        out_specs=P("row", "col"),
        check_vma=False,
    )
```

```python
import functools

import jax
import jax.numpy as jnp
from jax import lax
from jax.experimental import pallas as pl
from jax.experimental.pallas import tpu as pltpu
from jax.sharding import PartitionSpec as P

BLK = 128
GROUP = 16
CAP = 8


def slot_table(pattern):
    stored = (pattern > 0).astype(jnp.int32)
    rows = pattern.shape[0]
    groups = rows // GROUP
    grouped = stored.reshape(groups, GROUP, -1)
    slot = jnp.cumsum(grouped, axis=1) - 1
    group_base = (jnp.arange(groups, dtype=jnp.int32) * CAP)[:, None, None]
    slot = (slot + group_base).reshape(rows, -1)
    return stored, slot


def ring_gather(x, axis, index, count):
    pieces = [x]
    for k in range(1, count):
        perm = [(s, (s + k) % count) for s in range(count)]
        pieces.append(lax.ppermute(x, axis, perm))
    sources = [(index - k) % count for k in range(count)]
    return pieces, sources


def ring_gather_list(xs, axis, index, count):
    out, sources = [], []
    for x in xs:
        got, src = ring_gather(x, axis, index, count)
        out.extend(got)
        sources.extend(src)
    return out, sources


def product_kernel(slot_ref, rf_pos_ref, keep_ref, *refs, pieces, rf_groups, row_blocks, cols):
    left_refs = refs[:pieces]
    rf_refs = refs[pieces:pieces + rf_groups]
    out_ref = refs[pieces + rf_groups]
    lhs_scr, rf_scr, left_buf, sems = refs[pieces + rf_groups + 1:]
    per_group = pieces // rf_groups
    copies = [pltpu.make_async_copy(left_refs[p], left_buf.at[p], sems.at[p]) for p in range(pieces)]
    for c in copies:
        c.start()
    for q in range(pieces):
        at = pl.multiple_of(rf_pos_ref[q] * BLK, BLK)
        rf_scr[pl.ds(at, BLK), :] = rf_refs[q // per_group][q % per_group]
    for p in range(pieces):
        copies[p].wait()
        for i in range(row_blocks):
            s = slot_ref[p, i]
            blk = left_buf[p, jnp.maximum(s, 0)]
            blk = jnp.where(s >= 0, blk, jnp.zeros_like(blk))
            lhs_scr[i * BLK:(i + 1) * BLK, p * BLK:(p + 1) * BLK] = blk
    tile = 4 * BLK
    for t in range(row_blocks * BLK // tile):
        res = jnp.dot(
            lhs_scr[t * tile:(t + 1) * tile, :], rf_scr[...], preferred_element_type=jnp.float32
        )
        for a in range(tile // BLK):
            i = t * (tile // BLK) + a
            for b in range(cols // BLK):
                sub = res[a * BLK:(a + 1) * BLK, b * BLK:(b + 1) * BLK]
                sub = jnp.where(keep_ref[i, b] > 0, sub, jnp.zeros_like(sub))
                out_ref[i * BLK:(i + 1) * BLK, b * BLK:(b + 1) * BLK] = sub.astype(out_ref.dtype)


def product_call(slot_tbl, rf_pos, keep_patch, left_pieces, rf_pieces):
    pieces = len(left_pieces)
    rf_groups = len(rf_pieces)
    row_blocks = slot_tbl.shape[1]
    cols = rf_pieces[0].shape[-1]
    smem = pl.BlockSpec(memory_space=pltpu.SMEM)
    vmem = pl.BlockSpec(memory_space=pltpu.VMEM)
    flops = 2 * row_blocks * BLK * pieces * BLK * cols
    bytes_accessed = (
        pieces * left_pieces[0].size * 2 + rf_groups * rf_pieces[0].size * 2 + row_blocks * BLK * cols * 2
    )
    return pl.pallas_call(
        functools.partial(
            product_kernel, pieces=pieces, rf_groups=rf_groups, row_blocks=row_blocks, cols=cols
        ),
        out_shape=jax.ShapeDtypeStruct((row_blocks * BLK, cols), jnp.bfloat16),
        in_specs=[smem, smem, smem] + [pl.BlockSpec(memory_space=pl.ANY)] * pieces + [vmem] * rf_groups,
        out_specs=vmem,
        scratch_shapes=[
            pltpu.VMEM((row_blocks * BLK, pieces * BLK), jnp.bfloat16),
            pltpu.VMEM((pieces * BLK, cols), jnp.bfloat16),
            pltpu.VMEM((pieces,) + left_pieces[0].shape, left_pieces[0].dtype),
            pltpu.SemaphoreType.DMA((pieces,)),
        ],
        cost_estimate=pl.CostEstimate(flops=flops, bytes_accessed=bytes_accessed, transcendentals=0),
    )(slot_tbl, rf_pos, keep_patch, *left_pieces, *rf_pieces)


def per_device(left_matrix, square_term, block_pattern, keep_mask):
    row_idx = lax.axis_index("row")
    col_idx = lax.axis_index("col")
    layer_idx = lax.axis_index("layer")
    row_count = lax.axis_size("row")
    col_count = lax.axis_size("col")
    rows_local = left_matrix.shape[0]
    row_blocks = rows_local // BLK
    inner_blocks = left_matrix.shape[1] // BLK
    inner_local = square_term.shape[0]
    cols_local = square_term.shape[1]
    col_blocks = cols_local // BLK
    slots = (row_blocks // GROUP) * CAP
    total_inner_blocks = block_pattern.shape[1]

    inner_start = (layer_idx * col_count + col_idx) * inner_blocks
    pattern_patch = lax.dynamic_slice(
        block_pattern, (row_idx * row_blocks, inner_start), (row_blocks, inner_blocks)
    )
    stored, slot = slot_table(pattern_patch)
    slot_ids = jnp.arange(slots, dtype=jnp.int32)
    hit = (stored[:, :, None] > 0) & (slot[:, :, None] == slot_ids[None, None, :])
    source_row = jnp.sum(
        jnp.where(hit, jnp.arange(row_blocks, dtype=jnp.int32)[:, None, None], 0), axis=0
    )
    blocks = left_matrix.reshape(row_blocks, BLK, inner_blocks, BLK).transpose(2, 0, 1, 3)
    flat_blocks = blocks.reshape(inner_blocks * row_blocks, BLK, BLK)
    take_idx = source_row + (jnp.arange(inner_blocks, dtype=jnp.int32) * row_blocks)[:, None]
    packed = jnp.take(flat_blocks, take_idx.reshape(-1), axis=0)
    packed = packed.reshape(inner_blocks, slots, BLK, BLK)

    layer_count = lax.axis_size("layer")
    keep_patch = lax.dynamic_slice(
        keep_mask, (row_idx * row_blocks, col_idx * col_blocks), (row_blocks, col_blocks)
    ).astype(jnp.int32)
    panel_pattern = lax.dynamic_slice(
        block_pattern, (row_idx * row_blocks, 0), (row_blocks, total_inner_blocks)
    )

    first_inner = (layer_idx * row_count + row_idx) * inner_local
    first_col = col_idx * cols_local
    inner_pos = first_inner + lax.broadcasted_iota(jnp.int32, (inner_local, cols_local), 0)
    col_pos = first_col + lax.broadcasted_iota(jnp.int32, (inner_local, cols_local), 1)
    unit = jnp.where(inner_pos == col_pos, jnp.float32(1.5), jnp.float32(0.0))
    right_factor = (unit - 0.5 * square_term.astype(jnp.float32)).astype(jnp.bfloat16)

    use_permutes = (
        inner_blocks == 1
        and inner_local == BLK
        and col_count == row_count
        and col_count <= 4
        and layer_count <= 2
    )
    if use_permutes:
        rf_pair, rf_layer_src = ring_gather(right_factor, "layer", layer_idx, layer_count)
        rf_pair = jnp.stack(rf_pair)
        own_over_layer = [
            lax.ppermute(packed[0], "layer", [(s, (s + m) % layer_count) for s in range(layer_count)])
            for m in range(1, layer_count)
        ]
        def col_shift(x, k):
            return lax.ppermute(x, "col", [(s, (s + k) % col_count) for s in range(col_count)])

        col_pieces = {1: col_shift(packed[0], 1)}
        piece_layer = [(layer_idx - m) % layer_count for k in range(col_count) for m in range(layer_count)]
        piece_src_col = [(col_idx - k) % col_count for k in range(col_count) for m in range(layer_count)]
        piece_j = jnp.stack(
            [src_l * col_count + src_c for src_l, src_c in zip(piece_layer, piece_src_col)]
        ).astype(jnp.int32)
        rf_row = [(row_idx - k) % row_count for k in range(row_count) for m in range(layer_count)]
        rf_layer = [(layer_idx - m) % layer_count for k in range(row_count) for m in range(layer_count)]
        rf_q = jnp.stack([src_l * row_count + src_r for src_l, src_r in zip(rf_layer, rf_row)])
        rf_pos = ((col_idx - rf_q % col_count) % col_count) * layer_count + (
            (layer_idx - rf_q // col_count) % layer_count
        )
        p_stored, p_slot = slot_table(panel_pattern)
        slot_tbl = jnp.where(p_stored > 0, p_slot, -1).astype(jnp.int32)
        slot_tbl = jnp.take(slot_tbl, piece_j, axis=1).T
        later, col_pieces[1], slot_tbl, rf_pos, keep_patch, own_over_layer = lax.optimization_barrier(
            (packed[0], col_pieces[1], slot_tbl, rf_pos.astype(jnp.int32), keep_patch, own_over_layer)
        )
        for k in range(2, col_count):
            col_pieces[k] = col_shift(later, k)
        piece_col = [(col_idx - k) % col_count for k in range(col_count)]
        pieces = [packed[0]] + own_over_layer
        for k in range(1, col_count):
            got, _ = ring_gather(col_pieces[k], "layer", layer_idx, layer_count)
            pieces.extend(got)
        rf_pieces, _ = ring_gather(rf_pair, "row", row_idx, row_count)
        return product_call(slot_tbl, rf_pos, keep_patch, pieces, rf_pieces)

    gathered = lax.all_gather(packed, ("layer", "col"), axis=0, tiled=True)
    piece_j = jnp.arange(total_inner_blocks, dtype=jnp.int32)
    right_full = lax.all_gather(right_factor, ("layer", "row"), axis=0, tiled=True)

    p_stored, p_slot = slot_table(panel_pattern)
    p_stored = jnp.take(p_stored, piece_j, axis=1)
    p_slot = jnp.take(p_slot, piece_j, axis=1)
    gather_idx = (
        jnp.arange(total_inner_blocks, dtype=jnp.int32)[None, :] * slots
        + jnp.clip(p_slot, 0, slots - 1)
    )
    flat_packed = gathered.reshape(total_inner_blocks * slots, BLK, BLK)
    right_blocks = jnp.take(right_full.reshape(total_inner_blocks, BLK, cols_local), piece_j, axis=0)

    def chunk_sum(first, count):
        idx = lax.dynamic_slice_in_dim(gather_idx, first, count, axis=1)
        keep = lax.dynamic_slice_in_dim(p_stored, first, count, axis=1)
        dense = jnp.take(flat_packed, idx.reshape(-1), axis=0)
        dense = dense.reshape(row_blocks, count, BLK, BLK)
        dense = jnp.where(keep[:, :, None, None] > 0, dense, jnp.zeros_like(dense))
        rhs = lax.dynamic_slice_in_dim(right_blocks, first, count, axis=0)
        return jnp.einsum("ijab,jbc->iac", dense, rhs, preferred_element_type=jnp.float32)

    dense_bytes = row_blocks * total_inner_blocks * BLK * BLK * 2
    chunks = max(1, dense_bytes // (4 << 20))
    while total_inner_blocks % chunks:
        chunks += 1
    if chunks == 1:
        full_sum = chunk_sum(0, total_inner_blocks)
    else:
        per_chunk = total_inner_blocks // chunks

        def body(c, acc):
            return acc + chunk_sum(c * per_chunk, per_chunk)

        full_sum = lax.fori_loop(
            0, chunks, body, jnp.zeros((row_blocks, BLK, cols_local), jnp.float32)
        )
    full_sum = full_sum.reshape(rows_local, cols_local)

    keep_full = jnp.repeat(jnp.repeat(keep_patch, BLK, axis=0), BLK, axis=1)
    kept = jnp.where(keep_full > 0, full_sum, jnp.zeros_like(full_sum))
    return kept.astype(jnp.bfloat16)


def solution(mesh):
    return jax.shard_map(
        per_device,
        mesh=mesh,
        in_specs=(P("row", ("layer", "col")), P(("layer", "row"), "col"), P(), P()),
        out_specs=P("row", "col"),
        check_vma=False,
    )
```

```python
import functools

import jax
import jax.numpy as jnp
from jax import lax
from jax.experimental import pallas as pl
from jax.experimental.pallas import tpu as pltpu
from jax.sharding import PartitionSpec as P

BLK = 128
GROUP = 16
CAP = 8


def slot_table(pattern):
    stored = (pattern > 0).astype(jnp.int32)
    rows = pattern.shape[0]
    groups = rows // GROUP
    grouped = stored.reshape(groups, GROUP, -1)
    slot = jnp.cumsum(grouped, axis=1) - 1
    group_base = (jnp.arange(groups, dtype=jnp.int32) * CAP)[:, None, None]
    slot = (slot + group_base).reshape(rows, -1)
    return stored, slot


def ring_gather(x, axis, index, count):
    pieces = [x]
    for k in range(1, count):
        perm = [(s, (s + k) % count) for s in range(count)]
        pieces.append(lax.ppermute(x, axis, perm))
    sources = [(index - k) % count for k in range(count)]
    return pieces, sources


def ring_gather_list(xs, axis, index, count):
    out, sources = [], []
    for x in xs:
        got, src = ring_gather(x, axis, index, count)
        out.extend(got)
        sources.extend(src)
    return out, sources


def product_kernel(slot_ref, rf_pos_ref, keep_ref, *refs, pieces, rf_groups, row_blocks, cols):
    left_refs = refs[:pieces]
    rf_refs = refs[pieces:pieces + rf_groups]
    out_ref = refs[pieces + rf_groups]
    lhs_scr, rf_scr = refs[pieces + rf_groups + 1:]
    per_group = pieces // rf_groups
    for q in range(pieces):
        at = pl.multiple_of(rf_pos_ref[q] * BLK, BLK)
        rf_scr[pl.ds(at, BLK), :] = rf_refs[q // per_group][q % per_group]
    for p in range(pieces):
        for i in range(row_blocks):
            s = slot_ref[p, i]
            blk = left_refs[p][jnp.clip(s, 0, left_refs[p].shape[0] - 1)]
            blk = jnp.where(s >= 0, blk, jnp.zeros_like(blk))
            lhs_scr[i * BLK:(i + 1) * BLK, p * BLK:(p + 1) * BLK] = blk
    tile = 4 * BLK
    for t in range(row_blocks * BLK // tile):
        res = jnp.dot(
            lhs_scr[t * tile:(t + 1) * tile, :], rf_scr[...], preferred_element_type=jnp.float32
        )
        for a in range(tile // BLK):
            i = t * (tile // BLK) + a
            for b in range(cols // BLK):
                sub = res[a * BLK:(a + 1) * BLK, b * BLK:(b + 1) * BLK]
                sub = jnp.where(keep_ref[i, b] > 0, sub, jnp.zeros_like(sub))
                out_ref[i * BLK:(i + 1) * BLK, b * BLK:(b + 1) * BLK] = sub.astype(out_ref.dtype)


def product_call(slot_tbl, rf_pos, keep_patch, left_pieces, rf_pieces):
    pieces = len(left_pieces)
    rf_groups = len(rf_pieces)
    row_blocks = slot_tbl.shape[1]
    cols = rf_pieces[0].shape[-1]
    smem = pl.BlockSpec(memory_space=pltpu.SMEM)
    vmem = pl.BlockSpec(memory_space=pltpu.VMEM)
    flops = 2 * row_blocks * BLK * pieces * BLK * cols
    bytes_accessed = (
        pieces * left_pieces[0].size * 2 + rf_groups * rf_pieces[0].size * 2 + row_blocks * BLK * cols * 2
    )
    return pl.pallas_call(
        functools.partial(
            product_kernel, pieces=pieces, rf_groups=rf_groups, row_blocks=row_blocks, cols=cols
        ),
        out_shape=jax.ShapeDtypeStruct((row_blocks * BLK, cols), jnp.bfloat16),
        in_specs=[smem, smem, smem] + [vmem] * (pieces + rf_groups),
        out_specs=vmem,
        scratch_shapes=[
            pltpu.VMEM((row_blocks * BLK, pieces * BLK), jnp.bfloat16),
            pltpu.VMEM((pieces * BLK, cols), jnp.bfloat16),
        ],
        cost_estimate=pl.CostEstimate(flops=flops, bytes_accessed=bytes_accessed, transcendentals=0),
    )(slot_tbl, rf_pos, keep_patch, *left_pieces, *rf_pieces)


def per_device(left_matrix, square_term, block_pattern, keep_mask):
    row_idx = lax.axis_index("row")
    col_idx = lax.axis_index("col")
    layer_idx = lax.axis_index("layer")
    row_count = lax.axis_size("row")
    col_count = lax.axis_size("col")
    rows_local = left_matrix.shape[0]
    row_blocks = rows_local // BLK
    inner_blocks = left_matrix.shape[1] // BLK
    inner_local = square_term.shape[0]
    cols_local = square_term.shape[1]
    col_blocks = cols_local // BLK
    slots = (row_blocks // GROUP) * CAP
    total_inner_blocks = block_pattern.shape[1]

    inner_start = (layer_idx * col_count + col_idx) * inner_blocks
    pattern_patch = lax.dynamic_slice(
        block_pattern, (row_idx * row_blocks, inner_start), (row_blocks, inner_blocks)
    )
    stored, slot = slot_table(pattern_patch)
    slot_ids = jnp.arange(slots, dtype=jnp.int32)
    hit = (stored[:, :, None] > 0) & (slot[:, :, None] == slot_ids[None, None, :])
    source_row = jnp.sum(
        jnp.where(hit, jnp.arange(row_blocks, dtype=jnp.int32)[:, None, None], 0), axis=0
    )
    blocks = left_matrix.reshape(row_blocks, BLK, inner_blocks, BLK).transpose(2, 0, 1, 3)
    flat_blocks = blocks.reshape(inner_blocks * row_blocks, BLK, BLK)
    take_idx = source_row + (jnp.arange(inner_blocks, dtype=jnp.int32) * row_blocks)[:, None]
    packed = jnp.take(flat_blocks, take_idx.reshape(-1), axis=0)
    packed = packed.reshape(inner_blocks, slots, BLK, BLK)

    layer_count = lax.axis_size("layer")
    keep_patch = lax.dynamic_slice(
        keep_mask, (row_idx * row_blocks, col_idx * col_blocks), (row_blocks, col_blocks)
    ).astype(jnp.int32)
    panel_pattern = lax.dynamic_slice(
        block_pattern, (row_idx * row_blocks, 0), (row_blocks, total_inner_blocks)
    )

    first_inner = (layer_idx * row_count + row_idx) * inner_local
    first_col = col_idx * cols_local
    inner_pos = first_inner + lax.broadcasted_iota(jnp.int32, (inner_local, cols_local), 0)
    col_pos = first_col + lax.broadcasted_iota(jnp.int32, (inner_local, cols_local), 1)
    unit = jnp.where(inner_pos == col_pos, jnp.float32(1.5), jnp.float32(0.0))
    right_factor = (unit - 0.5 * square_term.astype(jnp.float32)).astype(jnp.bfloat16)

    use_permutes = (
        inner_blocks == 1
        and inner_local == BLK
        and col_count == row_count
        and col_count <= 4
        and layer_count <= 2
    )
    if use_permutes:
        rf_pair, rf_layer_src = ring_gather(right_factor, "layer", layer_idx, layer_count)
        rf_pair = jnp.stack(rf_pair)
        own_over_layer = [
            lax.ppermute(packed[0], "layer", [(s, (s + m) % layer_count) for s in range(layer_count)])
            for m in range(1, layer_count)
        ]
        def col_shift(x, k):
            return lax.ppermute(x, "col", [(s, (s + k) % col_count) for s in range(col_count)])

        col_pieces = {1: col_shift(packed[0], 1)}
        piece_layer = [(layer_idx - m) % layer_count for k in range(col_count) for m in range(layer_count)]
        piece_src_col = [(col_idx - k) % col_count for k in range(col_count) for m in range(layer_count)]
        piece_j = jnp.stack(
            [src_l * col_count + src_c for src_l, src_c in zip(piece_layer, piece_src_col)]
        ).astype(jnp.int32)
        rf_row = [(row_idx - k) % row_count for k in range(row_count) for m in range(layer_count)]
        rf_layer = [(layer_idx - m) % layer_count for k in range(row_count) for m in range(layer_count)]
        rf_q = jnp.stack([src_l * row_count + src_r for src_l, src_r in zip(rf_layer, rf_row)])
        rf_pos = ((col_idx - rf_q % col_count) % col_count) * layer_count + (
            (layer_idx - rf_q // col_count) % layer_count
        )
        p_stored, p_slot = slot_table(panel_pattern)
        slot_tbl = jnp.where(p_stored > 0, p_slot, -1).astype(jnp.int32)
        slot_tbl = jnp.take(slot_tbl, piece_j, axis=1).T
        later, col_pieces[1], slot_tbl, rf_pos, keep_patch, own_over_layer = lax.optimization_barrier(
            (packed[0], col_pieces[1], slot_tbl, rf_pos.astype(jnp.int32), keep_patch, own_over_layer)
        )
        for k in range(2, col_count):
            col_pieces[k] = col_shift(later, k)
        piece_col = [(col_idx - k) % col_count for k in range(col_count)]
        pieces = [packed[0]] + own_over_layer
        for k in range(1, col_count):
            got, _ = ring_gather(col_pieces[k], "layer", layer_idx, layer_count)
            pieces.extend(got)
        rf_pieces, _ = ring_gather(rf_pair, "row", row_idx, row_count)
        return product_call(slot_tbl, rf_pos, keep_patch, pieces, rf_pieces)

    gathered = lax.all_gather(packed, ("layer", "col"), axis=0, tiled=True)
    piece_j = jnp.arange(total_inner_blocks, dtype=jnp.int32)
    right_full = lax.all_gather(right_factor, ("layer", "row"), axis=0, tiled=True)

    p_stored, p_slot = slot_table(panel_pattern)
    p_stored = jnp.take(p_stored, piece_j, axis=1)
    p_slot = jnp.take(p_slot, piece_j, axis=1)
    gather_idx = (
        jnp.arange(total_inner_blocks, dtype=jnp.int32)[None, :] * slots
        + jnp.clip(p_slot, 0, slots - 1)
    )
    flat_packed = gathered.reshape(total_inner_blocks * slots, BLK, BLK)
    right_blocks = jnp.take(right_full.reshape(total_inner_blocks, BLK, cols_local), piece_j, axis=0)

    def chunk_sum(first, count):
        idx = lax.dynamic_slice_in_dim(gather_idx, first, count, axis=1)
        keep = lax.dynamic_slice_in_dim(p_stored, first, count, axis=1)
        dense = jnp.take(flat_packed, idx.reshape(-1), axis=0)
        dense = dense.reshape(row_blocks, count, BLK, BLK)
        dense = jnp.where(keep[:, :, None, None] > 0, dense, jnp.zeros_like(dense))
        rhs = lax.dynamic_slice_in_dim(right_blocks, first, count, axis=0)
        return jnp.einsum("ijab,jbc->iac", dense, rhs, preferred_element_type=jnp.float32)

    dense_bytes = row_blocks * total_inner_blocks * BLK * BLK * 2
    chunks = max(1, dense_bytes // (4 << 20))
    while total_inner_blocks % chunks:
        chunks += 1
    if chunks == 1:
        full_sum = chunk_sum(0, total_inner_blocks)
    else:
        per_chunk = total_inner_blocks // chunks

        def body(c, acc):
            return acc + chunk_sum(c * per_chunk, per_chunk)

        full_sum = lax.fori_loop(
            0, chunks, body, jnp.zeros((row_blocks, BLK, cols_local), jnp.float32)
        )
    full_sum = full_sum.reshape(rows_local, cols_local)

    keep_full = jnp.repeat(jnp.repeat(keep_patch, BLK, axis=0), BLK, axis=1)
    kept = jnp.where(keep_full > 0, full_sum, jnp.zeros_like(full_sum))
    return kept.astype(jnp.bfloat16)


def solution(mesh):
    return jax.shard_map(
        per_device,
        mesh=mesh,
        in_specs=(P("row", ("layer", "col")), P(("layer", "row"), "col"), P(), P()),
        out_specs=P("row", "col"),
        check_vma=False,
    )
```

```python
import functools

import jax
import jax.numpy as jnp
from jax import lax
from jax.experimental import pallas as pl
from jax.experimental.pallas import tpu as pltpu
from jax.sharding import PartitionSpec as P

BLK = 128
GROUP = 16
CAP = 8


def slot_table(pattern):
    stored = (pattern > 0).astype(jnp.int32)
    rows = pattern.shape[0]
    groups = rows // GROUP
    grouped = stored.reshape(groups, GROUP, -1)
    slot = jnp.cumsum(grouped, axis=1) - 1
    group_base = (jnp.arange(groups, dtype=jnp.int32) * CAP)[:, None, None]
    slot = (slot + group_base).reshape(rows, -1)
    return stored, slot


def ring_gather(x, axis, index, count):
    pieces = [x]
    for k in range(1, count):
        perm = [(s, (s + k) % count) for s in range(count)]
        pieces.append(lax.ppermute(x, axis, perm))
    sources = [(index - k) % count for k in range(count)]
    return pieces, sources


def ring_gather_list(xs, axis, index, count):
    out, sources = [], []
    for x in xs:
        got, src = ring_gather(x, axis, index, count)
        out.extend(got)
        sources.extend(src)
    return out, sources


def product_kernel(slot_ref, rf_pos_ref, keep_ref, *refs, pieces, rf_groups, row_blocks, cols):
    left_refs = refs[:pieces]
    rf_refs = refs[pieces:pieces + rf_groups]
    out_ref = refs[pieces + rf_groups]
    lhs_scr, rf_scr = refs[pieces + rf_groups + 1:]
    per_group = pieces // rf_groups
    for q in range(pieces):
        at = pl.multiple_of(rf_pos_ref[q] * BLK, BLK)
        rf_scr[pl.ds(at, BLK), :] = rf_refs[q // per_group][q % per_group]
    for p in range(pieces):
        for i in range(row_blocks):
            s = slot_ref[p, i]
            blk = left_refs[p][jnp.clip(s, 0, left_refs[p].shape[0] - 1)]
            blk = jnp.where(s >= 0, blk, jnp.zeros_like(blk))
            lhs_scr[i * BLK:(i + 1) * BLK, p * BLK:(p + 1) * BLK] = blk
    tile = 4 * BLK
    for t in range(row_blocks * BLK // tile):
        res = jnp.dot(
            lhs_scr[t * tile:(t + 1) * tile, :], rf_scr[...], preferred_element_type=jnp.float32
        )
        for a in range(tile // BLK):
            i = t * (tile // BLK) + a
            for b in range(cols // BLK):
                sub = res[a * BLK:(a + 1) * BLK, b * BLK:(b + 1) * BLK]
                sub = jnp.where(keep_ref[i, b] > 0, sub, jnp.zeros_like(sub))
                out_ref[i * BLK:(i + 1) * BLK, b * BLK:(b + 1) * BLK] = sub.astype(out_ref.dtype)


def product_call(slot_tbl, rf_pos, keep_patch, left_pieces, rf_pieces):
    pieces = len(left_pieces)
    rf_groups = len(rf_pieces)
    row_blocks = slot_tbl.shape[1]
    cols = rf_pieces[0].shape[-1]
    smem = pl.BlockSpec(memory_space=pltpu.SMEM)
    vmem = pl.BlockSpec(memory_space=pltpu.VMEM)
    flops = 2 * row_blocks * BLK * pieces * BLK * cols
    bytes_accessed = (
        pieces * left_pieces[0].size * 2 + rf_groups * rf_pieces[0].size * 2 + row_blocks * BLK * cols * 2
    )
    return pl.pallas_call(
        functools.partial(
            product_kernel, pieces=pieces, rf_groups=rf_groups, row_blocks=row_blocks, cols=cols
        ),
        out_shape=jax.ShapeDtypeStruct((row_blocks * BLK, cols), jnp.bfloat16),
        in_specs=[smem, smem, smem] + [vmem] * (pieces + rf_groups),
        out_specs=vmem,
        scratch_shapes=[
            pltpu.VMEM((row_blocks * BLK, pieces * BLK), jnp.bfloat16),
            pltpu.VMEM((pieces * BLK, cols), jnp.bfloat16),
        ],
        cost_estimate=pl.CostEstimate(flops=flops, bytes_accessed=bytes_accessed, transcendentals=0),
    )(slot_tbl, rf_pos, keep_patch, *left_pieces, *rf_pieces)


def per_device(left_matrix, square_term, block_pattern, keep_mask):
    row_idx = lax.axis_index("row")
    col_idx = lax.axis_index("col")
    layer_idx = lax.axis_index("layer")
    row_count = lax.axis_size("row")
    col_count = lax.axis_size("col")
    rows_local = left_matrix.shape[0]
    row_blocks = rows_local // BLK
    inner_blocks = left_matrix.shape[1] // BLK
    inner_local = square_term.shape[0]
    cols_local = square_term.shape[1]
    col_blocks = cols_local // BLK
    slots = (row_blocks // GROUP) * CAP
    total_inner_blocks = block_pattern.shape[1]

    inner_start = (layer_idx * col_count + col_idx) * inner_blocks
    pattern_patch = lax.dynamic_slice(
        block_pattern, (row_idx * row_blocks, inner_start), (row_blocks, inner_blocks)
    )
    stored, slot = slot_table(pattern_patch)
    slot_ids = jnp.arange(slots, dtype=jnp.int32)
    hit = (stored[:, :, None] > 0) & (slot[:, :, None] == slot_ids[None, None, :])
    source_row = jnp.sum(
        jnp.where(hit, jnp.arange(row_blocks, dtype=jnp.int32)[:, None, None], 0), axis=0
    )
    blocks = left_matrix.reshape(row_blocks, BLK, inner_blocks, BLK).transpose(2, 0, 1, 3)
    flat_blocks = blocks.reshape(inner_blocks * row_blocks, BLK, BLK)
    take_idx = source_row + (jnp.arange(inner_blocks, dtype=jnp.int32) * row_blocks)[:, None]
    packed = jnp.take(flat_blocks, take_idx.reshape(-1), axis=0)
    packed = packed.reshape(inner_blocks, slots, BLK, BLK)

    layer_count = lax.axis_size("layer")
    keep_patch = lax.dynamic_slice(
        keep_mask, (row_idx * row_blocks, col_idx * col_blocks), (row_blocks, col_blocks)
    ).astype(jnp.int32)
    panel_pattern = lax.dynamic_slice(
        block_pattern, (row_idx * row_blocks, 0), (row_blocks, total_inner_blocks)
    )

    first_inner = (layer_idx * row_count + row_idx) * inner_local
    first_col = col_idx * cols_local
    inner_pos = first_inner + lax.broadcasted_iota(jnp.int32, (inner_local, cols_local), 0)
    col_pos = first_col + lax.broadcasted_iota(jnp.int32, (inner_local, cols_local), 1)
    unit = jnp.where(inner_pos == col_pos, jnp.float32(1.5), jnp.float32(0.0))
    right_factor = (unit - 0.5 * square_term.astype(jnp.float32)).astype(jnp.bfloat16)

    use_permutes = (
        inner_blocks == 1
        and inner_local == BLK
        and col_count == row_count
        and col_count <= 4
        and layer_count <= 2
    )
    if use_permutes:
        rf_pair, rf_layer_src = ring_gather(right_factor, "layer", layer_idx, layer_count)
        rf_pair = jnp.stack(rf_pair)
        own_piece, rf_pair = lax.optimization_barrier((packed[0], rf_pair))
        own_over_layer = [
            lax.ppermute(own_piece, "layer", [(s, (s + m) % layer_count) for s in range(layer_count)])
            for m in range(1, layer_count)
        ]
        def col_shift(x, k):
            return lax.ppermute(x, "col", [(s, (s + k) % col_count) for s in range(col_count)])

        col_pieces = {1: col_shift(own_piece, 1)}
        piece_layer = [(layer_idx - m) % layer_count for k in range(col_count) for m in range(layer_count)]
        piece_src_col = [(col_idx - k) % col_count for k in range(col_count) for m in range(layer_count)]
        piece_j = jnp.stack(
            [src_l * col_count + src_c for src_l, src_c in zip(piece_layer, piece_src_col)]
        ).astype(jnp.int32)
        rf_row = [(row_idx - k) % row_count for k in range(row_count) for m in range(layer_count)]
        rf_layer = [(layer_idx - m) % layer_count for k in range(row_count) for m in range(layer_count)]
        rf_q = jnp.stack([src_l * row_count + src_r for src_l, src_r in zip(rf_layer, rf_row)])
        rf_pos = ((col_idx - rf_q % col_count) % col_count) * layer_count + (
            (layer_idx - rf_q // col_count) % layer_count
        )
        p_stored, p_slot = slot_table(panel_pattern)
        slot_tbl = jnp.where(p_stored > 0, p_slot, -1).astype(jnp.int32)
        slot_tbl = jnp.take(slot_tbl, piece_j, axis=1).T
        rf_pieces, _ = ring_gather(rf_pair, "row", row_idx, row_count)
        later, col_pieces[1], slot_tbl, rf_pos, keep_patch, own_over_layer, rf_pieces = (
            lax.optimization_barrier(
                (own_piece, col_pieces[1], slot_tbl, rf_pos.astype(jnp.int32), keep_patch, own_over_layer, rf_pieces)
            )
        )
        for k in range(2, col_count):
            col_pieces[k] = col_shift(later, k)
        piece_col = [(col_idx - k) % col_count for k in range(col_count)]
        pieces = [packed[0]] + own_over_layer
        for k in range(1, col_count):
            got, _ = ring_gather(col_pieces[k], "layer", layer_idx, layer_count)
            pieces.extend(got)
        return product_call(slot_tbl, rf_pos, keep_patch, pieces, rf_pieces)

    gathered = lax.all_gather(packed, ("layer", "col"), axis=0, tiled=True)
    piece_j = jnp.arange(total_inner_blocks, dtype=jnp.int32)
    right_full = lax.all_gather(right_factor, ("layer", "row"), axis=0, tiled=True)

    p_stored, p_slot = slot_table(panel_pattern)
    p_stored = jnp.take(p_stored, piece_j, axis=1)
    p_slot = jnp.take(p_slot, piece_j, axis=1)
    gather_idx = (
        jnp.arange(total_inner_blocks, dtype=jnp.int32)[None, :] * slots
        + jnp.clip(p_slot, 0, slots - 1)
    )
    flat_packed = gathered.reshape(total_inner_blocks * slots, BLK, BLK)
    right_blocks = jnp.take(right_full.reshape(total_inner_blocks, BLK, cols_local), piece_j, axis=0)

    def chunk_sum(first, count):
        idx = lax.dynamic_slice_in_dim(gather_idx, first, count, axis=1)
        keep = lax.dynamic_slice_in_dim(p_stored, first, count, axis=1)
        dense = jnp.take(flat_packed, idx.reshape(-1), axis=0)
        dense = dense.reshape(row_blocks, count, BLK, BLK)
        dense = jnp.where(keep[:, :, None, None] > 0, dense, jnp.zeros_like(dense))
        rhs = lax.dynamic_slice_in_dim(right_blocks, first, count, axis=0)
        return jnp.einsum("ijab,jbc->iac", dense, rhs, preferred_element_type=jnp.float32)

    dense_bytes = row_blocks * total_inner_blocks * BLK * BLK * 2
    chunks = max(1, dense_bytes // (4 << 20))
    while total_inner_blocks % chunks:
        chunks += 1
    if chunks == 1:
        full_sum = chunk_sum(0, total_inner_blocks)
    else:
        per_chunk = total_inner_blocks // chunks

        def body(c, acc):
            return acc + chunk_sum(c * per_chunk, per_chunk)

        full_sum = lax.fori_loop(
            0, chunks, body, jnp.zeros((row_blocks, BLK, cols_local), jnp.float32)
        )
    full_sum = full_sum.reshape(rows_local, cols_local)

    keep_full = jnp.repeat(jnp.repeat(keep_patch, BLK, axis=0), BLK, axis=1)
    kept = jnp.where(keep_full > 0, full_sum, jnp.zeros_like(full_sum))
    return kept.astype(jnp.bfloat16)


def solution(mesh):
    return jax.shard_map(
        per_device,
        mesh=mesh,
        in_specs=(P("row", ("layer", "col")), P(("layer", "row"), "col"), P(), P()),
        out_specs=P("row", "col"),
        check_vma=False,
    )
```

```python
import functools

import jax
import jax.numpy as jnp
from jax import lax
from jax.experimental import pallas as pl
from jax.experimental.pallas import tpu as pltpu
from jax.sharding import PartitionSpec as P

BLK = 128
GROUP = 16
CAP = 8


def slot_table(pattern):
    stored = (pattern > 0).astype(jnp.int32)
    rows = pattern.shape[0]
    groups = rows // GROUP
    grouped = stored.reshape(groups, GROUP, -1)
    slot = jnp.cumsum(grouped, axis=1) - 1
    group_base = (jnp.arange(groups, dtype=jnp.int32) * CAP)[:, None, None]
    slot = (slot + group_base).reshape(rows, -1)
    return stored, slot


def ring_gather(x, axis, index, count):
    pieces = [x]
    for k in range(1, count):
        perm = [(s, (s + k) % count) for s in range(count)]
        pieces.append(lax.ppermute(x, axis, perm))
    sources = [(index - k) % count for k in range(count)]
    return pieces, sources


def ring_gather_list(xs, axis, index, count):
    out, sources = [], []
    for x in xs:
        got, src = ring_gather(x, axis, index, count)
        out.extend(got)
        sources.extend(src)
    return out, sources


def product_kernel(slot_ref, rf_pos_ref, keep_ref, *refs, pieces, rf_groups, rf_entries, row_blocks, cols):
    left_refs = refs[:pieces]
    rf_refs = refs[pieces:pieces + rf_groups]
    out_ref = refs[pieces + rf_groups]
    lhs_scr, rf_scr = refs[pieces + rf_groups + 1:]
    for q, (ref_id, entry) in enumerate(rf_entries):
        at = pl.multiple_of(rf_pos_ref[q] * BLK, BLK)
        rf_scr[pl.ds(at, BLK), :] = rf_refs[ref_id][entry]
    for p in range(pieces):
        for i in range(row_blocks):
            s = slot_ref[p, i]
            blk = left_refs[p][jnp.clip(s, 0, left_refs[p].shape[0] - 1)]
            blk = jnp.where(s >= 0, blk, jnp.zeros_like(blk))
            lhs_scr[i * BLK:(i + 1) * BLK, p * BLK:(p + 1) * BLK] = blk
    tile = 4 * BLK
    for t in range(row_blocks * BLK // tile):
        res = jnp.dot(
            lhs_scr[t * tile:(t + 1) * tile, :], rf_scr[...], preferred_element_type=jnp.float32
        )
        for a in range(tile // BLK):
            i = t * (tile // BLK) + a
            for b in range(cols // BLK):
                sub = res[a * BLK:(a + 1) * BLK, b * BLK:(b + 1) * BLK]
                sub = jnp.where(keep_ref[i, b] > 0, sub, jnp.zeros_like(sub))
                out_ref[i * BLK:(i + 1) * BLK, b * BLK:(b + 1) * BLK] = sub.astype(out_ref.dtype)


def product_call(slot_tbl, rf_pos, keep_patch, left_pieces, rf_pieces, rf_entries):
    pieces = len(left_pieces)
    rf_groups = len(rf_pieces)
    row_blocks = slot_tbl.shape[1]
    cols = rf_pieces[0].shape[-1]
    smem = pl.BlockSpec(memory_space=pltpu.SMEM)
    vmem = pl.BlockSpec(memory_space=pltpu.VMEM)
    flops = 2 * row_blocks * BLK * pieces * BLK * cols
    bytes_accessed = (
        pieces * left_pieces[0].size * 2 + rf_groups * rf_pieces[0].size * 2 + row_blocks * BLK * cols * 2
    )
    return pl.pallas_call(
        functools.partial(
            product_kernel,
            pieces=pieces,
            rf_groups=rf_groups,
            rf_entries=tuple(rf_entries),
            row_blocks=row_blocks,
            cols=cols,
        ),
        out_shape=jax.ShapeDtypeStruct((row_blocks * BLK, cols), jnp.bfloat16),
        in_specs=[smem, smem, smem] + [vmem] * (pieces + rf_groups),
        out_specs=vmem,
        scratch_shapes=[
            pltpu.VMEM((row_blocks * BLK, pieces * BLK), jnp.bfloat16),
            pltpu.VMEM((pieces * BLK, cols), jnp.bfloat16),
        ],
        cost_estimate=pl.CostEstimate(flops=flops, bytes_accessed=bytes_accessed, transcendentals=0),
    )(slot_tbl, rf_pos, keep_patch, *left_pieces, *rf_pieces)


def per_device(left_matrix, square_term, block_pattern, keep_mask):
    row_idx = lax.axis_index("row")
    col_idx = lax.axis_index("col")
    layer_idx = lax.axis_index("layer")
    row_count = lax.axis_size("row")
    col_count = lax.axis_size("col")
    rows_local = left_matrix.shape[0]
    row_blocks = rows_local // BLK
    inner_blocks = left_matrix.shape[1] // BLK
    inner_local = square_term.shape[0]
    cols_local = square_term.shape[1]
    col_blocks = cols_local // BLK
    slots = (row_blocks // GROUP) * CAP
    total_inner_blocks = block_pattern.shape[1]

    inner_start = (layer_idx * col_count + col_idx) * inner_blocks
    pattern_patch = lax.dynamic_slice(
        block_pattern, (row_idx * row_blocks, inner_start), (row_blocks, inner_blocks)
    )
    stored, slot = slot_table(pattern_patch)
    slot_ids = jnp.arange(slots, dtype=jnp.int32)
    hit = (stored[:, :, None] > 0) & (slot[:, :, None] == slot_ids[None, None, :])
    source_row = jnp.sum(
        jnp.where(hit, jnp.arange(row_blocks, dtype=jnp.int32)[:, None, None], 0), axis=0
    )
    blocks = left_matrix.reshape(row_blocks, BLK, inner_blocks, BLK).transpose(2, 0, 1, 3)
    flat_blocks = blocks.reshape(inner_blocks * row_blocks, BLK, BLK)
    take_idx = source_row + (jnp.arange(inner_blocks, dtype=jnp.int32) * row_blocks)[:, None]
    packed = jnp.take(flat_blocks, take_idx.reshape(-1), axis=0)
    packed = packed.reshape(inner_blocks, slots, BLK, BLK)

    layer_count = lax.axis_size("layer")
    keep_patch = lax.dynamic_slice(
        keep_mask, (row_idx * row_blocks, col_idx * col_blocks), (row_blocks, col_blocks)
    ).astype(jnp.int32)
    panel_pattern = lax.dynamic_slice(
        block_pattern, (row_idx * row_blocks, 0), (row_blocks, total_inner_blocks)
    )

    first_inner = (layer_idx * row_count + row_idx) * inner_local
    first_col = col_idx * cols_local
    inner_pos = first_inner + lax.broadcasted_iota(jnp.int32, (inner_local, cols_local), 0)
    col_pos = first_col + lax.broadcasted_iota(jnp.int32, (inner_local, cols_local), 1)
    unit = jnp.where(inner_pos == col_pos, jnp.float32(1.5), jnp.float32(0.0))
    right_factor = (unit - 0.5 * square_term.astype(jnp.float32)).astype(jnp.bfloat16)

    use_permutes = (
        inner_blocks == 1
        and inner_local == BLK
        and col_count == row_count
        and col_count <= 4
        and layer_count <= 2
    )
    if use_permutes:
        rf_pair, rf_layer_src = ring_gather(right_factor, "layer", layer_idx, layer_count)
        rf_pair = jnp.stack(rf_pair)
        own_over_layer = [
            lax.ppermute(packed[0], "layer", [(s, (s + m) % layer_count) for s in range(layer_count)])
            for m in range(1, layer_count)
        ]
        def col_shift(x, k):
            return lax.ppermute(x, "col", [(s, (s + k) % col_count) for s in range(col_count)])

        col_pieces = {1: col_shift(packed[0], 1)}
        piece_layer = [(layer_idx - m) % layer_count for k in range(col_count) for m in range(layer_count)]
        piece_src_col = [(col_idx - k) % col_count for k in range(col_count) for m in range(layer_count)]
        piece_j = jnp.stack(
            [src_l * col_count + src_c for src_l, src_c in zip(piece_layer, piece_src_col)]
        ).astype(jnp.int32)
        rf_row = [q // layer_count for q in range(row_count * layer_count)]
        rf_layer = [(layer_idx - q % layer_count) % layer_count for q in range(row_count * layer_count)]
        rf_q = jnp.stack([src_l * row_count + src_r for src_l, src_r in zip(rf_layer, rf_row)])
        rf_pos = ((col_idx - rf_q % col_count) % col_count) * layer_count + (
            (layer_idx - rf_q // col_count) % layer_count
        )
        p_stored, p_slot = slot_table(panel_pattern)
        slot_tbl = jnp.where(p_stored > 0, p_slot, -1).astype(jnp.int32)
        slot_tbl = jnp.take(slot_tbl, piece_j, axis=1).T
        later, col_pieces[1], slot_tbl, rf_pos, keep_patch, own_over_layer = lax.optimization_barrier(
            (packed[0], col_pieces[1], slot_tbl, rf_pos.astype(jnp.int32), keep_patch, own_over_layer)
        )
        for k in range(2, col_count):
            col_pieces[k] = col_shift(later, k)
        piece_col = [(col_idx - k) % col_count for k in range(col_count)]
        pieces = [packed[0]] + own_over_layer
        for k in range(1, col_count):
            got, _ = ring_gather(col_pieces[k], "layer", layer_idx, layer_count)
            pieces.extend(got)
        padded = jnp.concatenate([rf_pair, jnp.zeros_like(rf_pair)], axis=0)
        rf_gathered = lax.all_gather(padded, "row", axis=0, tiled=True)
        rf_entries = [(0, (q // layer_count) * 2 * layer_count + q % layer_count)
                      for q in range(row_count * layer_count)]
        return product_call(slot_tbl, rf_pos, keep_patch, pieces, [rf_gathered], rf_entries)

    gathered = lax.all_gather(packed, ("layer", "col"), axis=0, tiled=True)
    piece_j = jnp.arange(total_inner_blocks, dtype=jnp.int32)
    right_full = lax.all_gather(right_factor, ("layer", "row"), axis=0, tiled=True)

    p_stored, p_slot = slot_table(panel_pattern)
    p_stored = jnp.take(p_stored, piece_j, axis=1)
    p_slot = jnp.take(p_slot, piece_j, axis=1)
    gather_idx = (
        jnp.arange(total_inner_blocks, dtype=jnp.int32)[None, :] * slots
        + jnp.clip(p_slot, 0, slots - 1)
    )
    flat_packed = gathered.reshape(total_inner_blocks * slots, BLK, BLK)
    right_blocks = jnp.take(right_full.reshape(total_inner_blocks, BLK, cols_local), piece_j, axis=0)

    def chunk_sum(first, count):
        idx = lax.dynamic_slice_in_dim(gather_idx, first, count, axis=1)
        keep = lax.dynamic_slice_in_dim(p_stored, first, count, axis=1)
        dense = jnp.take(flat_packed, idx.reshape(-1), axis=0)
        dense = dense.reshape(row_blocks, count, BLK, BLK)
        dense = jnp.where(keep[:, :, None, None] > 0, dense, jnp.zeros_like(dense))
        rhs = lax.dynamic_slice_in_dim(right_blocks, first, count, axis=0)
        return jnp.einsum("ijab,jbc->iac", dense, rhs, preferred_element_type=jnp.float32)

    dense_bytes = row_blocks * total_inner_blocks * BLK * BLK * 2
    chunks = max(1, dense_bytes // (4 << 20))
    while total_inner_blocks % chunks:
        chunks += 1
    if chunks == 1:
        full_sum = chunk_sum(0, total_inner_blocks)
    else:
        per_chunk = total_inner_blocks // chunks

        def body(c, acc):
            return acc + chunk_sum(c * per_chunk, per_chunk)

        full_sum = lax.fori_loop(
            0, chunks, body, jnp.zeros((row_blocks, BLK, cols_local), jnp.float32)
        )
    full_sum = full_sum.reshape(rows_local, cols_local)

    keep_full = jnp.repeat(jnp.repeat(keep_patch, BLK, axis=0), BLK, axis=1)
    kept = jnp.where(keep_full > 0, full_sum, jnp.zeros_like(full_sum))
    return kept.astype(jnp.bfloat16)


def solution(mesh):
    return jax.shard_map(
        per_device,
        mesh=mesh,
        in_specs=(P("row", ("layer", "col")), P(("layer", "row"), "col"), P(), P()),
        out_specs=P("row", "col"),
        check_vma=False,
    )
```

```python
import functools

import jax
import jax.numpy as jnp
from jax import lax
from jax.experimental import pallas as pl
from jax.experimental.pallas import tpu as pltpu
from jax.sharding import PartitionSpec as P

BLK = 128
GROUP = 16
CAP = 8


def slot_table(pattern):
    stored = (pattern > 0).astype(jnp.int32)
    rows = pattern.shape[0]
    groups = rows // GROUP
    grouped = stored.reshape(groups, GROUP, -1)
    slot = jnp.cumsum(grouped, axis=1) - 1
    group_base = (jnp.arange(groups, dtype=jnp.int32) * CAP)[:, None, None]
    slot = (slot + group_base).reshape(rows, -1)
    return stored, slot


def ring_gather(x, axis, index, count):
    pieces = [x]
    for k in range(1, count):
        perm = [(s, (s + k) % count) for s in range(count)]
        pieces.append(lax.ppermute(x, axis, perm))
    sources = [(index - k) % count for k in range(count)]
    return pieces, sources


def ring_gather_list(xs, axis, index, count):
    out, sources = [], []
    for x in xs:
        got, src = ring_gather(x, axis, index, count)
        out.extend(got)
        sources.extend(src)
    return out, sources


def product_kernel(slot_ref, rf_pos_ref, keep_ref, *refs, pieces, rf_groups, row_blocks, cols):
    left_refs = refs[:pieces]
    rf_refs = refs[pieces:pieces + rf_groups]
    out_ref = refs[pieces + rf_groups]
    lhs_scr, rf_scr, rf_buf, sems = refs[pieces + rf_groups + 1:]
    per_group = pieces // rf_groups
    copies = [pltpu.make_async_copy(rf_refs[g], rf_buf.at[g], sems.at[g]) for g in range(rf_groups)]
    for c in copies:
        c.start()
    for p in range(pieces):
        for i in range(row_blocks):
            s = slot_ref[p, i]
            blk = left_refs[p][jnp.clip(s, 0, left_refs[p].shape[0] - 1)]
            blk = jnp.where(s >= 0, blk, jnp.zeros_like(blk))
            lhs_scr[i * BLK:(i + 1) * BLK, p * BLK:(p + 1) * BLK] = blk
    for c in copies:
        c.wait()
    for q in range(pieces):
        at = pl.multiple_of(rf_pos_ref[q] * BLK, BLK)
        rf_scr[pl.ds(at, BLK), :] = rf_buf[q // per_group, q % per_group]
    tile = 4 * BLK
    for t in range(row_blocks * BLK // tile):
        res = jnp.dot(
            lhs_scr[t * tile:(t + 1) * tile, :], rf_scr[...], preferred_element_type=jnp.float32
        )
        for a in range(tile // BLK):
            i = t * (tile // BLK) + a
            for b in range(cols // BLK):
                sub = res[a * BLK:(a + 1) * BLK, b * BLK:(b + 1) * BLK]
                sub = jnp.where(keep_ref[i, b] > 0, sub, jnp.zeros_like(sub))
                out_ref[i * BLK:(i + 1) * BLK, b * BLK:(b + 1) * BLK] = sub.astype(out_ref.dtype)


def product_call(slot_tbl, rf_pos, keep_patch, left_pieces, rf_pieces):
    pieces = len(left_pieces)
    rf_groups = len(rf_pieces)
    row_blocks = slot_tbl.shape[1]
    cols = rf_pieces[0].shape[-1]
    smem = pl.BlockSpec(memory_space=pltpu.SMEM)
    vmem = pl.BlockSpec(memory_space=pltpu.VMEM)
    flops = 2 * row_blocks * BLK * pieces * BLK * cols
    bytes_accessed = (
        pieces * left_pieces[0].size * 2 + rf_groups * rf_pieces[0].size * 2 + row_blocks * BLK * cols * 2
    )
    return pl.pallas_call(
        functools.partial(
            product_kernel, pieces=pieces, rf_groups=rf_groups, row_blocks=row_blocks, cols=cols
        ),
        out_shape=jax.ShapeDtypeStruct((row_blocks * BLK, cols), jnp.bfloat16),
        in_specs=[smem, smem, smem] + [vmem] * pieces + [pl.BlockSpec(memory_space=pl.ANY)] * rf_groups,
        out_specs=vmem,
        scratch_shapes=[
            pltpu.VMEM((row_blocks * BLK, pieces * BLK), jnp.bfloat16),
            pltpu.VMEM((pieces * BLK, cols), jnp.bfloat16),
            pltpu.VMEM((rf_groups,) + rf_pieces[0].shape, rf_pieces[0].dtype),
            pltpu.SemaphoreType.DMA((rf_groups,)),
        ],
        cost_estimate=pl.CostEstimate(flops=flops, bytes_accessed=bytes_accessed, transcendentals=0),
    )(slot_tbl, rf_pos, keep_patch, *left_pieces, *rf_pieces)


def per_device(left_matrix, square_term, block_pattern, keep_mask):
    row_idx = lax.axis_index("row")
    col_idx = lax.axis_index("col")
    layer_idx = lax.axis_index("layer")
    row_count = lax.axis_size("row")
    col_count = lax.axis_size("col")
    rows_local = left_matrix.shape[0]
    row_blocks = rows_local // BLK
    inner_blocks = left_matrix.shape[1] // BLK
    inner_local = square_term.shape[0]
    cols_local = square_term.shape[1]
    col_blocks = cols_local // BLK
    slots = (row_blocks // GROUP) * CAP
    total_inner_blocks = block_pattern.shape[1]

    inner_start = (layer_idx * col_count + col_idx) * inner_blocks
    pattern_patch = lax.dynamic_slice(
        block_pattern, (row_idx * row_blocks, inner_start), (row_blocks, inner_blocks)
    )
    stored, slot = slot_table(pattern_patch)
    slot_ids = jnp.arange(slots, dtype=jnp.int32)
    hit = (stored[:, :, None] > 0) & (slot[:, :, None] == slot_ids[None, None, :])
    source_row = jnp.sum(
        jnp.where(hit, jnp.arange(row_blocks, dtype=jnp.int32)[:, None, None], 0), axis=0
    )
    blocks = left_matrix.reshape(row_blocks, BLK, inner_blocks, BLK).transpose(2, 0, 1, 3)
    flat_blocks = blocks.reshape(inner_blocks * row_blocks, BLK, BLK)
    take_idx = source_row + (jnp.arange(inner_blocks, dtype=jnp.int32) * row_blocks)[:, None]
    packed = jnp.take(flat_blocks, take_idx.reshape(-1), axis=0)
    packed = packed.reshape(inner_blocks, slots, BLK, BLK)

    layer_count = lax.axis_size("layer")
    keep_patch = lax.dynamic_slice(
        keep_mask, (row_idx * row_blocks, col_idx * col_blocks), (row_blocks, col_blocks)
    ).astype(jnp.int32)
    panel_pattern = lax.dynamic_slice(
        block_pattern, (row_idx * row_blocks, 0), (row_blocks, total_inner_blocks)
    )

    first_inner = (layer_idx * row_count + row_idx) * inner_local
    first_col = col_idx * cols_local
    inner_pos = first_inner + lax.broadcasted_iota(jnp.int32, (inner_local, cols_local), 0)
    col_pos = first_col + lax.broadcasted_iota(jnp.int32, (inner_local, cols_local), 1)
    unit = jnp.where(inner_pos == col_pos, jnp.float32(1.5), jnp.float32(0.0))
    right_factor = (unit - 0.5 * square_term.astype(jnp.float32)).astype(jnp.bfloat16)

    use_permutes = (
        inner_blocks == 1
        and inner_local == BLK
        and col_count == row_count
        and col_count <= 4
        and layer_count <= 2
    )
    if use_permutes:
        rf_pair, rf_layer_src = ring_gather(right_factor, "layer", layer_idx, layer_count)
        rf_pair = jnp.stack(rf_pair)
        own_over_layer = [
            lax.ppermute(packed[0], "layer", [(s, (s + m) % layer_count) for s in range(layer_count)])
            for m in range(1, layer_count)
        ]
        def col_shift(x, k):
            return lax.ppermute(x, "col", [(s, (s + k) % col_count) for s in range(col_count)])

        col_pieces = {1: col_shift(packed[0], 1)}
        piece_layer = [(layer_idx - m) % layer_count for k in range(col_count) for m in range(layer_count)]
        piece_src_col = [(col_idx - k) % col_count for k in range(col_count) for m in range(layer_count)]
        piece_j = jnp.stack(
            [src_l * col_count + src_c for src_l, src_c in zip(piece_layer, piece_src_col)]
        ).astype(jnp.int32)
        rf_row = [(row_idx - k) % row_count for k in range(row_count) for m in range(layer_count)]
        rf_layer = [(layer_idx - m) % layer_count for k in range(row_count) for m in range(layer_count)]
        rf_q = jnp.stack([src_l * row_count + src_r for src_l, src_r in zip(rf_layer, rf_row)])
        rf_pos = ((col_idx - rf_q % col_count) % col_count) * layer_count + (
            (layer_idx - rf_q // col_count) % layer_count
        )
        p_stored, p_slot = slot_table(panel_pattern)
        slot_tbl = jnp.where(p_stored > 0, p_slot, -1).astype(jnp.int32)
        slot_tbl = jnp.take(slot_tbl, piece_j, axis=1).T
        later, col_pieces[1], slot_tbl, rf_pos, keep_patch, own_over_layer = lax.optimization_barrier(
            (packed[0], col_pieces[1], slot_tbl, rf_pos.astype(jnp.int32), keep_patch, own_over_layer)
        )
        for k in range(2, col_count):
            col_pieces[k] = col_shift(later, k)
        piece_col = [(col_idx - k) % col_count for k in range(col_count)]
        pieces = [packed[0]] + own_over_layer
        for k in range(1, col_count):
            got, _ = ring_gather(col_pieces[k], "layer", layer_idx, layer_count)
            pieces.extend(got)
        rf_pieces, _ = ring_gather(rf_pair, "row", row_idx, row_count)
        return product_call(slot_tbl, rf_pos, keep_patch, pieces, rf_pieces)

    gathered = lax.all_gather(packed, ("layer", "col"), axis=0, tiled=True)
    piece_j = jnp.arange(total_inner_blocks, dtype=jnp.int32)
    right_full = lax.all_gather(right_factor, ("layer", "row"), axis=0, tiled=True)

    p_stored, p_slot = slot_table(panel_pattern)
    p_stored = jnp.take(p_stored, piece_j, axis=1)
    p_slot = jnp.take(p_slot, piece_j, axis=1)
    gather_idx = (
        jnp.arange(total_inner_blocks, dtype=jnp.int32)[None, :] * slots
        + jnp.clip(p_slot, 0, slots - 1)
    )
    flat_packed = gathered.reshape(total_inner_blocks * slots, BLK, BLK)
    right_blocks = jnp.take(right_full.reshape(total_inner_blocks, BLK, cols_local), piece_j, axis=0)

    def chunk_sum(first, count):
        idx = lax.dynamic_slice_in_dim(gather_idx, first, count, axis=1)
        keep = lax.dynamic_slice_in_dim(p_stored, first, count, axis=1)
        dense = jnp.take(flat_packed, idx.reshape(-1), axis=0)
        dense = dense.reshape(row_blocks, count, BLK, BLK)
        dense = jnp.where(keep[:, :, None, None] > 0, dense, jnp.zeros_like(dense))
        rhs = lax.dynamic_slice_in_dim(right_blocks, first, count, axis=0)
        return jnp.einsum("ijab,jbc->iac", dense, rhs, preferred_element_type=jnp.float32)

    dense_bytes = row_blocks * total_inner_blocks * BLK * BLK * 2
    chunks = max(1, dense_bytes // (4 << 20))
    while total_inner_blocks % chunks:
        chunks += 1
    if chunks == 1:
        full_sum = chunk_sum(0, total_inner_blocks)
    else:
        per_chunk = total_inner_blocks // chunks

        def body(c, acc):
            return acc + chunk_sum(c * per_chunk, per_chunk)

        full_sum = lax.fori_loop(
            0, chunks, body, jnp.zeros((row_blocks, BLK, cols_local), jnp.float32)
        )
    full_sum = full_sum.reshape(rows_local, cols_local)

    keep_full = jnp.repeat(jnp.repeat(keep_patch, BLK, axis=0), BLK, axis=1)
    kept = jnp.where(keep_full > 0, full_sum, jnp.zeros_like(full_sum))
    return kept.astype(jnp.bfloat16)


def solution(mesh):
    return jax.shard_map(
        per_device,
        mesh=mesh,
        in_specs=(P("row", ("layer", "col")), P(("layer", "row"), "col"), P(), P()),
        out_specs=P("row", "col"),
        check_vma=False,
    )
```

```python
import functools

import jax
import jax.numpy as jnp
from jax import lax
from jax.experimental import pallas as pl
from jax.experimental.pallas import tpu as pltpu
from jax.sharding import PartitionSpec as P

BLK = 128
GROUP = 16
CAP = 8


def slot_table(pattern):
    stored = (pattern > 0).astype(jnp.int32)
    rows = pattern.shape[0]
    groups = rows // GROUP
    grouped = stored.reshape(groups, GROUP, -1)
    slot = jnp.cumsum(grouped, axis=1) - 1
    group_base = (jnp.arange(groups, dtype=jnp.int32) * CAP)[:, None, None]
    slot = (slot + group_base).reshape(rows, -1)
    return stored, slot


def ring_gather(x, axis, index, count):
    pieces = [x]
    for k in range(1, count):
        perm = [(s, (s + k) % count) for s in range(count)]
        pieces.append(lax.ppermute(x, axis, perm))
    sources = [(index - k) % count for k in range(count)]
    return pieces, sources


def ring_gather_list(xs, axis, index, count):
    out, sources = [], []
    for x in xs:
        got, src = ring_gather(x, axis, index, count)
        out.extend(got)
        sources.extend(src)
    return out, sources


def product_kernel(slot_ref, rf_pos_ref, keep_ref, *refs, pieces, rf_groups, row_blocks, cols):
    left_refs = refs[:pieces]
    rf_refs = refs[pieces:pieces + rf_groups]
    out_ref = refs[pieces + rf_groups]
    lhs_scr, rf_scr = refs[pieces + rf_groups + 1:]
    per_group = pieces // rf_groups
    for q in range(pieces):
        at = pl.multiple_of(rf_pos_ref[q] * BLK, BLK)
        rf_scr[pl.ds(at, BLK), :] = rf_refs[q // per_group][q % per_group]
    for p in range(pieces):
        for i in range(row_blocks):
            s = slot_ref[p, i]
            blk = left_refs[p][jnp.clip(s, 0, left_refs[p].shape[0] - 1)]
            blk = jnp.where(s >= 0, blk, jnp.zeros_like(blk))
            lhs_scr[i * BLK:(i + 1) * BLK, p * BLK:(p + 1) * BLK] = blk
    tile = 8 * BLK
    for t in range(row_blocks * BLK // tile):
        res = jnp.dot(
            lhs_scr[t * tile:(t + 1) * tile, :], rf_scr[...], preferred_element_type=jnp.float32
        )
        for a in range(tile // BLK):
            i = t * (tile // BLK) + a
            for b in range(cols // BLK):
                sub = res[a * BLK:(a + 1) * BLK, b * BLK:(b + 1) * BLK]
                sub = jnp.where(keep_ref[i, b] > 0, sub, jnp.zeros_like(sub))
                out_ref[i * BLK:(i + 1) * BLK, b * BLK:(b + 1) * BLK] = sub.astype(out_ref.dtype)


def product_call(slot_tbl, rf_pos, keep_patch, left_pieces, rf_pieces):
    pieces = len(left_pieces)
    rf_groups = len(rf_pieces)
    row_blocks = slot_tbl.shape[1]
    cols = rf_pieces[0].shape[-1]
    smem = pl.BlockSpec(memory_space=pltpu.SMEM)
    vmem = pl.BlockSpec(memory_space=pltpu.VMEM)
    flops = 2 * row_blocks * BLK * pieces * BLK * cols
    bytes_accessed = (
        pieces * left_pieces[0].size * 2 + rf_groups * rf_pieces[0].size * 2 + row_blocks * BLK * cols * 2
    )
    return pl.pallas_call(
        functools.partial(
            product_kernel, pieces=pieces, rf_groups=rf_groups, row_blocks=row_blocks, cols=cols
        ),
        out_shape=jax.ShapeDtypeStruct((row_blocks * BLK, cols), jnp.bfloat16),
        in_specs=[smem, smem, smem] + [vmem] * (pieces + rf_groups),
        out_specs=vmem,
        scratch_shapes=[
            pltpu.VMEM((row_blocks * BLK, pieces * BLK), jnp.bfloat16),
            pltpu.VMEM((pieces * BLK, cols), jnp.bfloat16),
        ],
        cost_estimate=pl.CostEstimate(flops=flops, bytes_accessed=bytes_accessed, transcendentals=0),
    )(slot_tbl, rf_pos, keep_patch, *left_pieces, *rf_pieces)


def per_device(left_matrix, square_term, block_pattern, keep_mask):
    row_idx = lax.axis_index("row")
    col_idx = lax.axis_index("col")
    layer_idx = lax.axis_index("layer")
    row_count = lax.axis_size("row")
    col_count = lax.axis_size("col")
    rows_local = left_matrix.shape[0]
    row_blocks = rows_local // BLK
    inner_blocks = left_matrix.shape[1] // BLK
    inner_local = square_term.shape[0]
    cols_local = square_term.shape[1]
    col_blocks = cols_local // BLK
    slots = (row_blocks // GROUP) * CAP
    total_inner_blocks = block_pattern.shape[1]

    inner_start = (layer_idx * col_count + col_idx) * inner_blocks
    pattern_patch = lax.dynamic_slice(
        block_pattern, (row_idx * row_blocks, inner_start), (row_blocks, inner_blocks)
    )
    stored, slot = slot_table(pattern_patch)
    slot_ids = jnp.arange(slots, dtype=jnp.int32)
    hit = (stored[:, :, None] > 0) & (slot[:, :, None] == slot_ids[None, None, :])
    source_row = jnp.sum(
        jnp.where(hit, jnp.arange(row_blocks, dtype=jnp.int32)[:, None, None], 0), axis=0
    )
    blocks = left_matrix.reshape(row_blocks, BLK, inner_blocks, BLK).transpose(2, 0, 1, 3)
    flat_blocks = blocks.reshape(inner_blocks * row_blocks, BLK, BLK)
    take_idx = source_row + (jnp.arange(inner_blocks, dtype=jnp.int32) * row_blocks)[:, None]
    packed = jnp.take(flat_blocks, take_idx.reshape(-1), axis=0)
    packed = packed.reshape(inner_blocks, slots, BLK, BLK)

    layer_count = lax.axis_size("layer")
    keep_patch = lax.dynamic_slice(
        keep_mask, (row_idx * row_blocks, col_idx * col_blocks), (row_blocks, col_blocks)
    ).astype(jnp.int32)
    panel_pattern = lax.dynamic_slice(
        block_pattern, (row_idx * row_blocks, 0), (row_blocks, total_inner_blocks)
    )

    first_inner = (layer_idx * row_count + row_idx) * inner_local
    first_col = col_idx * cols_local
    inner_pos = first_inner + lax.broadcasted_iota(jnp.int32, (inner_local, cols_local), 0)
    col_pos = first_col + lax.broadcasted_iota(jnp.int32, (inner_local, cols_local), 1)
    unit = jnp.where(inner_pos == col_pos, jnp.float32(1.5), jnp.float32(0.0))
    right_factor = (unit - 0.5 * square_term.astype(jnp.float32)).astype(jnp.bfloat16)

    use_permutes = (
        inner_blocks == 1
        and inner_local == BLK
        and col_count == row_count
        and col_count <= 4
        and layer_count <= 2
    )
    if use_permutes:
        rf_pair, rf_layer_src = ring_gather(right_factor, "layer", layer_idx, layer_count)
        rf_pair = jnp.stack(rf_pair)
        own_over_layer = [
            lax.ppermute(packed[0], "layer", [(s, (s + m) % layer_count) for s in range(layer_count)])
            for m in range(1, layer_count)
        ]
        def col_shift(x, k):
            return lax.ppermute(x, "col", [(s, (s + k) % col_count) for s in range(col_count)])

        col_pieces = {1: col_shift(packed[0], 1)}
        piece_layer = [(layer_idx - m) % layer_count for k in range(col_count) for m in range(layer_count)]
        piece_src_col = [(col_idx - k) % col_count for k in range(col_count) for m in range(layer_count)]
        piece_j = jnp.stack(
            [src_l * col_count + src_c for src_l, src_c in zip(piece_layer, piece_src_col)]
        ).astype(jnp.int32)
        rf_row = [(row_idx - k) % row_count for k in range(row_count) for m in range(layer_count)]
        rf_layer = [(layer_idx - m) % layer_count for k in range(row_count) for m in range(layer_count)]
        rf_q = jnp.stack([src_l * row_count + src_r for src_l, src_r in zip(rf_layer, rf_row)])
        rf_pos = ((col_idx - rf_q % col_count) % col_count) * layer_count + (
            (layer_idx - rf_q // col_count) % layer_count
        )
        p_stored, p_slot = slot_table(panel_pattern)
        slot_tbl = jnp.where(p_stored > 0, p_slot, -1).astype(jnp.int32)
        slot_tbl = jnp.take(slot_tbl, piece_j, axis=1).T
        later, col_pieces[1], slot_tbl, rf_pos, keep_patch, own_over_layer = lax.optimization_barrier(
            (packed[0], col_pieces[1], slot_tbl, rf_pos.astype(jnp.int32), keep_patch, own_over_layer)
        )
        for k in range(2, col_count):
            col_pieces[k] = col_shift(later, k)
        piece_col = [(col_idx - k) % col_count for k in range(col_count)]
        pieces = [packed[0]] + own_over_layer
        for k in range(1, col_count):
            got, _ = ring_gather(col_pieces[k], "layer", layer_idx, layer_count)
            pieces.extend(got)
        rf_pieces, _ = ring_gather(rf_pair, "row", row_idx, row_count)
        return product_call(slot_tbl, rf_pos, keep_patch, pieces, rf_pieces)

    gathered = lax.all_gather(packed, ("layer", "col"), axis=0, tiled=True)
    piece_j = jnp.arange(total_inner_blocks, dtype=jnp.int32)
    right_full = lax.all_gather(right_factor, ("layer", "row"), axis=0, tiled=True)

    p_stored, p_slot = slot_table(panel_pattern)
    p_stored = jnp.take(p_stored, piece_j, axis=1)
    p_slot = jnp.take(p_slot, piece_j, axis=1)
    gather_idx = (
        jnp.arange(total_inner_blocks, dtype=jnp.int32)[None, :] * slots
        + jnp.clip(p_slot, 0, slots - 1)
    )
    flat_packed = gathered.reshape(total_inner_blocks * slots, BLK, BLK)
    right_blocks = jnp.take(right_full.reshape(total_inner_blocks, BLK, cols_local), piece_j, axis=0)

    def chunk_sum(first, count):
        idx = lax.dynamic_slice_in_dim(gather_idx, first, count, axis=1)
        keep = lax.dynamic_slice_in_dim(p_stored, first, count, axis=1)
        dense = jnp.take(flat_packed, idx.reshape(-1), axis=0)
        dense = dense.reshape(row_blocks, count, BLK, BLK)
        dense = jnp.where(keep[:, :, None, None] > 0, dense, jnp.zeros_like(dense))
        rhs = lax.dynamic_slice_in_dim(right_blocks, first, count, axis=0)
        return jnp.einsum("ijab,jbc->iac", dense, rhs, preferred_element_type=jnp.float32)

    dense_bytes = row_blocks * total_inner_blocks * BLK * BLK * 2
    chunks = max(1, dense_bytes // (4 << 20))
    while total_inner_blocks % chunks:
        chunks += 1
    if chunks == 1:
        full_sum = chunk_sum(0, total_inner_blocks)
    else:
        per_chunk = total_inner_blocks // chunks

        def body(c, acc):
            return acc + chunk_sum(c * per_chunk, per_chunk)

        full_sum = lax.fori_loop(
            0, chunks, body, jnp.zeros((row_blocks, BLK, cols_local), jnp.float32)
        )
    full_sum = full_sum.reshape(rows_local, cols_local)

    keep_full = jnp.repeat(jnp.repeat(keep_patch, BLK, axis=0), BLK, axis=1)
    kept = jnp.where(keep_full > 0, full_sum, jnp.zeros_like(full_sum))
    return kept.astype(jnp.bfloat16)


def solution(mesh):
    return jax.shard_map(
        per_device,
        mesh=mesh,
        in_specs=(P("row", ("layer", "col")), P(("layer", "row"), "col"), P(), P()),
        out_specs=P("row", "col"),
        check_vma=False,
    )
```
